512 devices in a mesh: group: 64 (over z, y), mp: 8 (over x, core).
Axes of the slice: x: 4, y: 8, z: 8, core: 2. Of those that a mesh axis runs over, the one named last changes fastest.
Arguments:
- tokens: bfloat16 [8192, 4096], P('group', 'mp'), may hold values from -3000 to 3000
- attn_gain: float32 [4096], replicated, may hold values from 0.1 to 1.9
- q_weight: bfloat16 [4096, 4096], P('group', 'mp'), may hold values from -0.09375 to 0.09375
- k_weight: bfloat16 [4096, 512], P('group'), may hold values from -0.09375 to 0.09375
- v_weight: bfloat16 [4096, 512], P('group'), may hold values from -0.09375 to 0.09375
- kv_pool: bfloat16 [4096, 8, 2, 16, 128], P('group', 'mp'), may hold values from -1000 to 1000
- page_table: int32 [256, 16], replicated, may hold values from 0 to 4095, as said below
- lengths: int32 [256], P('group'), may hold values from 2 to 256
- token_request: int32 [8192], P('group'), may hold values from 0 to 3
Outputs:
- attention: bfloat16 [8192, 4096], P('group', 'mp')
- decode_cache: bfloat16 [256, 8, 2, 256, 128], P('group', 'mp')
The draws below stay inside these ranges and needn't reach their ends.
Inputs may be any that keep to these rules, and one draw needn't show every extreme that they name: Every pool page stands in exactly one slot of page_table. The pages that one group index holds for the requests of one owner (requests o * 4 to (o + 1) * 4 - 1) number at most 2, and exactly 2 for some pairs of holder and owner.
All inputs are finite; a program needn't handle non-finite values.
Results may differ from the reference program's by a relative error of at most 0.038.
Values may be sent and summed in bfloat16 or wider, within the bound.
No kernel may reach another device: no remote copies, remote signals or barrier semaphores. Data moves between devices by JAX's collectives and lax.ppermute only.
A program may use at most 64 MiB of HBM per device.

```python
import math
import jax
import jax.numpy as jnp
import numpy as np
from jax import lax

D = 4096
HEADS = 32
KVH = 4
HD = 128
LAYERS = 2
PAGE = 16
SLOTS = 16
TOK_DEV = 128
REQ_DEV = 4
TOKENS = 8192
REQUESTS = 256
PAGES_DEV = 64
PAGES = 4096
MAXLEN = 256
LKV = 8


def draw_tokens(key, part):
    keys_all = jax.random.split(key, 3)
    columns = jnp.arange(D, dtype=jnp.float32)
    column_scale = 3.0 ** (columns / D) * jnp.exp(jax.random.uniform(keys_all[1], (D,), jnp.float32, 0.0, math.log(10.0)))
    base = jax.random.truncated_normal(keys_all[0], -6.0, 6.0, (TOKENS, D), jnp.float32)
    row_scale = jnp.exp(jax.random.uniform(keys_all[2], (TOKENS, 1), jnp.float32, 0.0, math.log(10.0)))
    return (base * row_scale * column_scale[None, :]).astype(jnp.bfloat16)


def draw_kv_pool(key, part):
    pool_shape = (PAGES, LAYERS * KVH, 2, PAGE, HD)
    keys_all = jax.random.split(key, 1)
    result = jax.random.truncated_normal(keys_all[0], -6.0, 6.0, pool_shape, jnp.float32)
    return result.astype(jnp.bfloat16)


def draw_page_table(key, part):
    group_count = REQUESTS // REQ_DEV
    per_device = PAGES_DEV
    mean_load = per_device // group_count
    keys_all = jax.random.split(key, 6)
    relabel_out = jax.random.permutation(keys_all[0], group_count)
    relabel_in = jax.random.permutation(keys_all[1], group_count)
    tier_index = jnp.arange(group_count)
    pattern = jnp.where(tier_index < group_count // 4, 2 * mean_load, jnp.where(tier_index < 3 * group_count // 4, mean_load, 0))
    pair_loads = pattern[jax.random.permutation(keys_all[2], group_count)]
    offsets = jnp.repeat(jnp.arange(group_count), pair_loads, total_repeat_length=per_device)
    offsets = offsets[jax.random.permutation(keys_all[3], per_device)]
    source_order = jax.vmap(lambda sub_key: jax.random.permutation(sub_key, per_device))(jax.random.split(keys_all[4], group_count))
    target_order = jax.vmap(lambda sub_key: jax.random.permutation(sub_key, per_device))(jax.random.split(keys_all[5], group_count))
    inverse_out = jnp.argsort(relabel_out)
    inverse_in = jnp.argsort(relabel_in)
    owners = jnp.arange(group_count)[:, None]
    senders = inverse_in[(inverse_out[owners] - offsets[None, :]) % group_count]
    rounds = jnp.arange(per_device)[None, :]
    pool_index = senders * per_device + source_order[senders, rounds]
    slot_index = owners * per_device + target_order
    page_lookup = jnp.zeros((group_count * per_device,), jnp.int32).at[slot_index.reshape(-1)].set(pool_index.reshape(-1).astype(jnp.int32))
    return page_lookup.reshape(REQUESTS, SLOTS)


def touch_ends(values, rng, least, top_value):
    dims = values.shape
    spot = [jax.random.randint(jax.random.fold_in(rng, axis), (), 0, dims[axis]) for axis in range(len(dims))]
    values = values.at[tuple(spot)].set(least)
    longest = dims.index(max(dims))
    spot[longest] = (spot[longest] + 1) % dims[longest]
    return values.at[tuple(spot)].set(top_value)


def block_scale(key, dims, cuts, low, high):
    factor_of = 1.0
    for dim, parts in cuts:
        draws = jax.random.uniform(jax.random.fold_in(jax.random.fold_in(key, 6), dim), (parts,), jnp.float32, low / len(cuts), high / len(cuts))
        factor_of = factor_of * jnp.repeat(jnp.exp(draws), dims[dim] // parts).reshape((-1,) + (1,) * (len(dims) - 1 - dim))
    return factor_of


def cumulative_ranks(amount, slope):
    portions = [(1 << 20) // math.isqrt(rank ** slope) + 1 for rank in range(1, amount + 1)]
    spread = 1 + sum(portions) // (1 << 30)
    return np.cumsum(np.array([max(1, weight // spread) for weight in portions]))


def skewed_ids(own_key, shape, amount, slope):
    table = cumulative_ranks(amount, slope)
    pick = jax.random.randint(jax.random.fold_in(own_key, 1), shape, 0, int(table[amount - 1]))
    rank = jnp.searchsorted(jnp.asarray(table, jnp.int32), pick, side="right")
    return jax.random.permutation(jax.random.fold_in(own_key, 2), amount)[rank].astype(jnp.int32)


def bell_draw(stream_key, shape, scale, bound, shards=(), held_as=jnp.bfloat16):
    gain = block_scale(stream_key, shape, shards, -0.22, 0.18) if shards else 1.0
    entries = jax.random.normal(stream_key, shape, jnp.float32) * scale * gain
    return jnp.minimum(jnp.maximum(entries, -bound), bound).astype(held_as)


def setup_inputs(seed: int = 0) -> dict:
    keys = jax.random.split(jax.random.key(seed), 10)
    tokens = draw_tokens(jax.random.fold_in(keys[9], 71), 0)
    attn_gain = jnp.clip(1.0 + 0.18 * jax.random.normal(keys[1], (D,), jnp.float32), 0.1, 1.9)
    q_weight = bell_draw(keys[2], (D, HEADS * HD), D ** -0.5, 0.09375, ((0, 64), (1, 8)))
    k_weight = bell_draw(keys[3], (D, KVH * HD), D ** -0.5, 0.09375, ((0, 64),))
    v_weight = bell_draw(keys[4], (D, KVH * HD), D ** -0.5, 0.09375, ((0, 64),))
    kv_pool = draw_kv_pool(jax.random.fold_in(keys[9], 71), 0)
    page_table = draw_page_table(jax.random.fold_in(keys[9], 71), 0)
    lengths = touch_ends(jax.random.randint(keys[7], (REQUESTS,), 2, MAXLEN + 1), jax.random.fold_in(keys[7], 1), 2, MAXLEN).astype(jnp.int32)
    token_request = touch_ends(skewed_ids(keys[8], (TOKENS,), REQ_DEV, 2), jax.random.fold_in(keys[8], 3), 0, REQ_DEV - 1).astype(jnp.int32)
    return dict(tokens=tokens, attn_gain=attn_gain, q_weight=q_weight, k_weight=k_weight, v_weight=v_weight, kv_pool=kv_pool, page_table=page_table, lengths=lengths, token_request=token_request)


rope_theta = 5000000.0
norm_eps = 1e-05

def rotate(vectors, position):
    half_dim = vectors.shape[-1] // 2
    frequency = rope_theta ** (-(jnp.arange(half_dim, dtype=jnp.float32) / half_dim))
    angles = position.astype(jnp.float32)[:, None, None] * frequency[None, None, :]
    cosine = jnp.cos(angles)
    sine_part = jnp.sin(angles)
    first_half = vectors[..., :half_dim]
    second = vectors[..., half_dim:]
    return jnp.concatenate([first_half * cosine - second * sine_part, second * cosine + first_half * sine_part], axis=-1)

def normalize(group_rows, attn_gain):
    features = group_rows.astype(jnp.float32)
    root_mean = jnp.sqrt(lax.optimization_barrier(jnp.mean(features * features, axis=-1, keepdims=True)) + norm_eps)
    return (features / root_mean * attn_gain.astype(jnp.float32)).astype(jnp.bfloat16)

def token_positions(token_request, group_lengths, request_count):
    member = (token_request[:, None] == jnp.arange(request_count, dtype=jnp.int32)[None, :]).astype(jnp.int32)
    earlier = lax.optimization_barrier(jnp.sum((jnp.cumsum(member, axis=0) - member) * member, axis=1))
    return lax.optimization_barrier(jnp.sum(member * group_lengths[None, :], axis=1)) + earlier

def build_mask(token_request, group_lengths, max_len):
    request_count = group_lengths.shape[0]
    key_index = jnp.arange(request_count * max_len, dtype=jnp.int32)
    key_request = key_index // max_len
    key_alive = key_index % max_len < group_lengths[key_request]
    cached = (token_request[:, None] == key_request[None, :]) & key_alive[None, :]
    token_order = jnp.arange(token_request.shape[0], dtype=jnp.int32)
    fresh = (token_request[:, None] == token_request[None, :]) & (token_order[None, :] <= token_order[:, None])
    return jnp.concatenate([cached, fresh], axis=1)

def weigh(scores, allowed):
    masked = jnp.where(allowed, scores, -1e+30)
    row_top = lax.optimization_barrier(jnp.max(masked, axis=-1, keepdims=True))
    exponent = jnp.exp(masked - row_top)
    return (exponent / lax.optimization_barrier(jnp.sum(exponent, axis=-1, keepdims=True))).astype(jnp.bfloat16)

def reference(tokens, attn_gain, q_weight, k_weight, v_weight, kv_pool, page_table, lengths, token_request):
    gathered = kv_pool[page_table]
    decoded = gathered.transpose(0, 2, 3, 1, 4, 5).reshape(REQUESTS, LKV, 2, MAXLEN, HD)
    alive_mask = jnp.arange(MAXLEN, dtype=jnp.int32)[None, :] < lengths[:, None]
    pool_order = jnp.where(alive_mask[:, None, None, :, None], decoded, jnp.zeros((), decoded.dtype))
    decode_cache = pool_order.reshape(REQUESTS, KVH, LAYERS, 2, MAXLEN, HD)[:, :, ::-1].reshape(REQUESTS, LKV, 2, MAXLEN, HD)
    group_count = REQUESTS // REQ_DEV
    per_kv = HEADS // KVH
    score_scale = HD ** (-0.5)

    def one_group(items):
        group_rows, requests_of, group_lengths, cache = items
        normed = normalize(group_rows, attn_gain)
        position = token_positions(requests_of, group_lengths, REQ_DEV)
        queries = jnp.dot(normed, q_weight, preferred_element_type=jnp.float32).reshape(TOK_DEV, HEADS, HD)
        queries = rotate(queries, position).astype(jnp.bfloat16)
        new_keys = jnp.dot(normed, k_weight, preferred_element_type=jnp.float32).reshape(TOK_DEV, KVH, HD)
        new_keys = rotate(new_keys, position).astype(jnp.bfloat16)
        new_values = jnp.dot(normed, v_weight, preferred_element_type=jnp.float32).astype(jnp.bfloat16).reshape(TOK_DEV, KVH, HD)
        layer_zero = cache[:, 0::LAYERS]
        cache_keys = layer_zero[:, :, 0].transpose(1, 0, 2, 3).reshape(KVH, REQ_DEV * MAXLEN, HD)
        cache_values = layer_zero[:, :, 1].transpose(1, 0, 2, 3).reshape(KVH, REQ_DEV * MAXLEN, HD)
        all_keys = jnp.concatenate([cache_keys, new_keys.transpose(1, 0, 2)], axis=1)
        all_values = jnp.concatenate([cache_values, new_values.transpose(1, 0, 2)], axis=1)
        allowed = build_mask(requests_of, group_lengths, MAXLEN)
        grouped = queries.reshape(TOK_DEV, KVH, per_kv, HD)
        scores = jnp.einsum('tkgd,knd->kgtn', grouped.astype(jnp.float32), all_keys.astype(jnp.float32)) * score_scale
        attn_probs = weigh(scores, allowed)
        mixture = jnp.einsum('kgtn,knd->tkgd', attn_probs.astype(jnp.float32), all_values.astype(jnp.float32))
        return mixture.astype(jnp.bfloat16).reshape(TOK_DEV, HEADS * HD)
    attention = lax.map(one_group, (tokens.reshape(group_count, TOK_DEV, D), token_request.reshape(group_count, TOK_DEV), lengths.reshape(group_count, REQ_DEV), pool_order.reshape(group_count, REQ_DEV, LKV, 2, MAXLEN, HD)))
    return (attention.reshape(TOKENS, HEADS * HD), decode_cache)
```

```python
import jax
import jax.numpy as jnp
from jax import lax
from jax.sharding import PartitionSpec as P

HEADS = 32
KVH = 4


rope_theta = 5000000.0
norm_eps = 1e-05


def from_partner(x, axis, bit):
    return lax.ppermute(x, axis, [(i, i ^ 1 << bit) for i in range(lax.axis_size(axis))])


def rotate(vectors, position):
    half_dim = vectors.shape[-1] // 2
    frequency = rope_theta ** (-(jnp.arange(half_dim, dtype=jnp.float32) / half_dim))
    angles = position.astype(jnp.float32)[:, None, None] * frequency[None, None, :]
    cosine = jnp.cos(angles)
    sine_part = jnp.sin(angles)
    first_half = vectors[..., :half_dim]
    second = vectors[..., half_dim:]
    return jnp.concatenate(
        [first_half * cosine - second * sine_part, second * cosine + first_half * sine_part],
        axis=-1,
    )


def normalize(group_rows, attn_gain):
    features = group_rows.astype(jnp.float32)
    root_mean = jnp.sqrt(jnp.mean(features * features, axis=-1, keepdims=True) + norm_eps)
    return (features / root_mean * attn_gain).astype(jnp.bfloat16)


def token_positions(token_request, group_lengths, request_count):
    member = (token_request[:, None] == jnp.arange(request_count, dtype=jnp.int32)[None, :]).astype(
        jnp.int32
    )
    earlier = jnp.sum((jnp.cumsum(member, axis=0) - member) * member, axis=1)
    return jnp.sum(member * group_lengths[None, :], axis=1) + earlier


def build_mask(token_request, group_lengths, max_len):
    request_count = group_lengths.shape[0]
    key_index = jnp.arange(request_count * max_len, dtype=jnp.int32)
    key_request = key_index // max_len
    key_alive = key_index % max_len < group_lengths[key_request]
    cached = (token_request[:, None] == key_request[None, :]) & key_alive[None, :]
    token_order = jnp.arange(token_request.shape[0], dtype=jnp.int32)
    fresh = (token_request[:, None] == token_request[None, :]) & (
        token_order[None, :] <= token_order[:, None]
    )
    return jnp.concatenate([cached, fresh], axis=1)


def weigh(scores, allowed):
    masked = jnp.where(allowed, scores, -1e30)
    row_top = jnp.max(masked, axis=-1, keepdims=True)
    exponent = jnp.exp(masked - row_top)
    return (exponent / jnp.sum(exponent, axis=-1, keepdims=True)).astype(jnp.bfloat16)


def on_device(
    tokens, attn_gain, q_weight, k_weight, v_weight, kv_pool, page_table, lengths, token_request
):
    groups = lax.axis_size("group")
    group_idx = lax.axis_index("group")
    mp_idx = lax.axis_index("mp")
    pool_pages = kv_pool.shape[0]
    pair_count = kv_pool.shape[1]
    page_len = kv_pool.shape[3]
    head_dim = kv_pool.shape[4]
    requests_here = lengths.shape[0]
    slot_count = pool_pages // requests_here
    max_len = slot_count * page_len
    capacity = 2 * pool_pages // groups
    flat_table = page_table.reshape(-1)
    slot_ids = jnp.arange(flat_table.shape[0], dtype=jnp.int32)
    owner_slot = jnp.zeros((flat_table.shape[0],), jnp.int32).at[flat_table].set(slot_ids)
    held_slots = lax.dynamic_slice_in_dim(owner_slot, group_idx * pool_pages, pool_pages)
    target_owner = held_slots // pool_pages
    slot_local = held_slots % pool_pages
    owner_hits = (target_owner[:, None] == jnp.arange(groups, dtype=jnp.int32)[None, :]).astype(
        jnp.int32
    )
    order_within = jnp.sum((jnp.cumsum(owner_hits, axis=0) - owner_hits) * owner_hits, axis=1)
    buffer_row = target_owner * capacity + order_within
    page_rows = kv_pool.reshape(pool_pages, -1)
    row_width = page_rows.shape[1]
    outgoing = (
        jnp.zeros((groups * capacity, row_width), jnp.bfloat16)
        .at[buffer_row]
        .set(page_rows)
        .reshape(groups, capacity, row_width)
    )
    outgoing_slots = (
        jnp.full((groups * capacity,), -1, jnp.int32)
        .at[buffer_row]
        .set(slot_local)
        .reshape(groups, capacity)
    )
    arrived, arrived_slots = (
        lax.all_to_all(outgoing, "group", split_axis=0, concat_axis=0, tiled=True),
        lax.all_to_all(outgoing_slots, "group", split_axis=0, concat_axis=0, tiled=True),
    )
    landing = jnp.where(arrived_slots < 0, pool_pages, arrived_slots).reshape(-1)
    placed = (
        jnp.zeros((pool_pages + 1, row_width), jnp.bfloat16)
        .at[landing]
        .set(arrived.reshape(-1, row_width))[:pool_pages]
    )
    decoded = placed.reshape(requests_here, slot_count, pair_count, 2, page_len, head_dim)
    decoded = decoded.transpose(0, 2, 3, 1, 4, 5).reshape(
        requests_here, pair_count, 2, max_len, head_dim
    )
    alive_mask = jnp.arange(max_len, dtype=jnp.int32)[None, :] < lengths[:, None]
    decoded = jnp.where(alive_mask[:, None, None, :, None], decoded, jnp.zeros((), jnp.bfloat16))
    whole_rows = lax.all_gather(tokens, "mp", axis=1, tiled=True)
    normed = normalize(whole_rows, attn_gain)
    rows_here = tokens.shape[0]
    heads_here = q_weight.shape[1] // head_dim
    per_kv = HEADS // KVH
    first_kv = mp_idx * heads_here // per_kv
    key_cols = lax.dynamic_slice_in_dim(k_weight, first_kv * head_dim, head_dim, 1)
    value_cols = lax.dynamic_slice_in_dim(v_weight, first_kv * head_dim, head_dim, 1)
    q_cols = q_weight.shape[1]
    joined_cols = jnp.concatenate([q_weight, key_cols, value_cols], axis=1)
    joined_sum = jnp.dot(
        normed,
        lax.all_gather(joined_cols, "group", axis=0, tiled=True),
        preferred_element_type=jnp.float32,
    )
    query_sum = joined_sum[:, :q_cols]
    key_sum = joined_sum[:, q_cols : q_cols + head_dim]
    value_sum = joined_sum[:, q_cols + head_dim :]
    position = token_positions(token_request, lengths, requests_here)
    queries = (
        rotate(query_sum.reshape(rows_here, heads_here, head_dim), position)
        .astype(jnp.bfloat16)
        .transpose(1, 0, 2)
    )
    new_keys = rotate(key_sum.reshape(rows_here, 1, head_dim), position).astype(jnp.bfloat16)[:, 0]
    new_values = value_sum.astype(jnp.bfloat16)
    allowed = build_mask(token_request, lengths, max_len)
    score_scale = head_dim ** (-0.5)
    partner_cache = from_partner(decoded, "mp", 0)
    is_even = mp_idx % 2 == 0
    layer_zero = jnp.where(is_even, decoded, partner_cache)[:, 0]
    all_keys = jnp.concatenate(
        [layer_zero[:, 0].reshape(requests_here * max_len, head_dim), new_keys], axis=0
    )
    all_values = jnp.concatenate(
        [layer_zero[:, 1].reshape(requests_here * max_len, head_dim), new_values], axis=0
    )

    def attend(query_one):
        scores = (
            jnp.einsum("td,nd->tn", query_one, all_keys, preferred_element_type=jnp.float32)
            * score_scale
        )
        attn_probs = weigh(scores, allowed)
        return jnp.dot(attn_probs, all_values, preferred_element_type=jnp.float32).astype(
            jnp.bfloat16
        )

    heads_out = lax.map(attend, queries)
    attention = heads_out.transpose(1, 0, 2).reshape(rows_here, heads_here * head_dim)
    return (attention, partner_cache)


def solution(mesh):
    return jax.shard_map(
        on_device,
        mesh=mesh,
        in_specs=(
            P("group", "mp"),
            P(),
            P("group", "mp"),
            P("group", None),
            P("group", None),
            P("group", "mp", None, None, None),
            P(),
            P("group"),
            P("group"),
        ),
        out_specs=(P("group", "mp"), P("group", "mp", None, None, None)),
        check_vma=False,
    )
```

```python
import jax
import jax.numpy as jnp
from jax import lax
from jax.sharding import Mesh, PartitionSpec as P

HEADS = 32
KVH = 4
GROUP = ("gz", "gy")


rope_theta = 5000000.0
norm_eps = 1e-05


def from_partner(x, axis, bit):
    return lax.ppermute(x, axis, [(i, i ^ 1 << bit) for i in range(lax.axis_size(axis))])


def rotate(vectors, position):
    half_dim = vectors.shape[-1] // 2
    frequency = rope_theta ** (-(jnp.arange(half_dim, dtype=jnp.float32) / half_dim))
    angles = position.astype(jnp.float32)[:, None, None] * frequency[None, None, :]
    cosine = jnp.cos(angles)
    sine_part = jnp.sin(angles)
    first_half = vectors[..., :half_dim]
    second = vectors[..., half_dim:]
    return jnp.concatenate(
        [first_half * cosine - second * sine_part, second * cosine + first_half * sine_part],
        axis=-1,
    )


def normalize(group_rows, attn_gain):
    features = group_rows.astype(jnp.float32)
    root_mean = jnp.sqrt(jnp.mean(features * features, axis=-1, keepdims=True) + norm_eps)
    return (features / root_mean * attn_gain).astype(jnp.bfloat16)


def token_positions(token_request, group_lengths, request_count):
    member = (token_request[:, None] == jnp.arange(request_count, dtype=jnp.int32)[None, :]).astype(
        jnp.int32
    )
    earlier = jnp.sum((jnp.cumsum(member, axis=0) - member) * member, axis=1)
    return jnp.sum(member * group_lengths[None, :], axis=1) + earlier


def build_mask(token_request, group_lengths, max_len):
    request_count = group_lengths.shape[0]
    key_index = jnp.arange(request_count * max_len, dtype=jnp.int32)
    key_request = key_index // max_len
    key_alive = key_index % max_len < group_lengths[key_request]
    cached = (token_request[:, None] == key_request[None, :]) & key_alive[None, :]
    token_order = jnp.arange(token_request.shape[0], dtype=jnp.int32)
    fresh = (token_request[:, None] == token_request[None, :]) & (
        token_order[None, :] <= token_order[:, None]
    )
    return jnp.concatenate([cached, fresh], axis=1)


def weigh(scores, allowed):
    masked = jnp.where(allowed, scores, -1e30)
    row_top = jnp.max(masked, axis=-1, keepdims=True)
    exponent = jnp.exp(masked - row_top)
    return (exponent / jnp.sum(exponent, axis=-1, keepdims=True)).astype(jnp.bfloat16)


def on_device(
    tokens, attn_gain, q_weight, k_weight, v_weight, kv_pool, page_table, lengths, token_request
):
    groups = lax.axis_size(GROUP)
    group_idx = lax.axis_index(GROUP)
    mp_idx = lax.axis_index("mp")
    pool_pages = kv_pool.shape[0]
    pair_count = kv_pool.shape[1]
    page_len = kv_pool.shape[3]
    head_dim = kv_pool.shape[4]
    requests_here = lengths.shape[0]
    slot_count = pool_pages // requests_here
    max_len = slot_count * page_len
    capacity = 2 * pool_pages // groups
    flat_table = page_table.reshape(-1)
    slot_ids = jnp.arange(flat_table.shape[0], dtype=jnp.int32)
    owner_slot = jnp.zeros((flat_table.shape[0],), jnp.int32).at[flat_table].set(slot_ids)
    held_slots = lax.dynamic_slice_in_dim(owner_slot, group_idx * pool_pages, pool_pages)
    target_owner = held_slots // pool_pages
    slot_local = held_slots % pool_pages
    owner_hits = (target_owner[:, None] == jnp.arange(groups, dtype=jnp.int32)[None, :]).astype(
        jnp.int32
    )
    order_within = jnp.sum((jnp.cumsum(owner_hits, axis=0) - owner_hits) * owner_hits, axis=1)
    buffer_row = target_owner * capacity + order_within
    page_rows = kv_pool.reshape(pool_pages, -1)
    row_width = page_rows.shape[1]
    outgoing = (
        jnp.zeros((groups * capacity, row_width), jnp.bfloat16)
        .at[buffer_row]
        .set(page_rows)
        .reshape(groups, capacity, row_width)
    )
    outgoing_slots = (
        jnp.full((groups * capacity,), -1, jnp.int32)
        .at[buffer_row]
        .set(slot_local)
        .reshape(groups, capacity)
    )
    arrived, arrived_slots = (
        lax.all_to_all(outgoing, GROUP, split_axis=0, concat_axis=0, tiled=True),
        lax.all_to_all(outgoing_slots, GROUP, split_axis=0, concat_axis=0, tiled=True),
    )
    landing = jnp.where(arrived_slots < 0, pool_pages, arrived_slots).reshape(-1)
    placed = (
        jnp.zeros((pool_pages + 1, row_width), jnp.bfloat16)
        .at[landing]
        .set(arrived.reshape(-1, row_width))[:pool_pages]
    )
    decoded = placed.reshape(requests_here, slot_count, pair_count, 2, page_len, head_dim)
    decoded = decoded.transpose(0, 2, 3, 1, 4, 5).reshape(
        requests_here, pair_count, 2, max_len, head_dim
    )
    alive_mask = jnp.arange(max_len, dtype=jnp.int32)[None, :] < lengths[:, None]
    decoded = jnp.where(alive_mask[:, None, None, :, None], decoded, jnp.zeros((), jnp.bfloat16))
    whole_rows = lax.all_gather(tokens, "mp", axis=1, tiled=True)
    normed = normalize(whole_rows, attn_gain)
    rows_here = tokens.shape[0]
    heads_here = q_weight.shape[1] // head_dim
    per_kv = HEADS // KVH
    first_kv = mp_idx * heads_here // per_kv
    key_cols = lax.dynamic_slice_in_dim(k_weight, first_kv * head_dim, head_dim, 1)
    value_cols = lax.dynamic_slice_in_dim(v_weight, first_kv * head_dim, head_dim, 1)
    q_cols = q_weight.shape[1]
    joined_cols = jnp.concatenate([q_weight, key_cols, value_cols], axis=1)
    joined_sum = jnp.dot(
        normed,
        lax.all_gather(
            lax.all_gather(joined_cols, "gy", axis=0, tiled=True), "gz", axis=0, tiled=True
        ),
        preferred_element_type=jnp.float32,
    )
    query_sum = joined_sum[:, :q_cols]
    key_sum = joined_sum[:, q_cols : q_cols + head_dim]
    value_sum = joined_sum[:, q_cols + head_dim :]
    position = token_positions(token_request, lengths, requests_here)
    queries = (
        rotate(query_sum.reshape(rows_here, heads_here, head_dim), position)
        .astype(jnp.bfloat16)
        .transpose(1, 0, 2)
    )
    new_keys = rotate(key_sum.reshape(rows_here, 1, head_dim), position).astype(jnp.bfloat16)[:, 0]
    new_values = value_sum.astype(jnp.bfloat16)
    allowed = build_mask(token_request, lengths, max_len)
    score_scale = head_dim ** (-0.5)
    partner_cache = from_partner(decoded, "mp", 0)
    is_even = mp_idx % 2 == 0
    layer_zero = jnp.where(is_even, decoded, partner_cache)[:, 0]
    all_keys = jnp.concatenate(
        [layer_zero[:, 0].reshape(requests_here * max_len, head_dim), new_keys], axis=0
    )
    all_values = jnp.concatenate(
        [layer_zero[:, 1].reshape(requests_here * max_len, head_dim), new_values], axis=0
    )

    def attend(query_one):
        scores = (
            jnp.einsum("td,nd->tn", query_one, all_keys, preferred_element_type=jnp.float32)
            * score_scale
        )
        attn_probs = weigh(scores, allowed)
        return jnp.dot(attn_probs, all_values, preferred_element_type=jnp.float32).astype(
            jnp.bfloat16
        )

    heads_out = lax.map(attend, queries)
    attention = heads_out.transpose(1, 0, 2).reshape(rows_here, heads_here * head_dim)
    return (attention, partner_cache)


def split_mesh(mesh):
    devices = mesh.devices
    groups, parts = devices.shape
    try:
        z_of = [d.coords[2] for d in devices[:, 0]]
        inner = next((i for i in range(1, groups) if z_of[i] != z_of[0]), groups)
    except (AttributeError, IndexError, TypeError):
        inner = int(round(groups**0.5))
    return Mesh(devices.reshape(groups // inner, inner, parts), ("gz", "gy", "mp"))


def solution(mesh):
    return jax.shard_map(
        on_device,
        mesh=split_mesh(mesh),
        in_specs=(
            P(GROUP, "mp"),
            P(),
            P(GROUP, "mp"),
            P(GROUP, None),
            P(GROUP, None),
            P(GROUP, "mp", None, None, None),
            P(),
            P(GROUP),
            P(GROUP),
        ),
        out_specs=(P(GROUP, "mp"), P(GROUP, "mp", None, None, None)),
        check_vma=False,
    )
```

```python
import jax
import jax.numpy as jnp
from jax import lax
from jax.sharding import Mesh, PartitionSpec as P

HEADS = 32
KVH = 4
GROUP = ("gz", "gy")


rope_theta = 5000000.0
norm_eps = 1e-05


def from_partner(x, axis, bit):
    return lax.ppermute(x, axis, [(i, i ^ 1 << bit) for i in range(lax.axis_size(axis))])


def gather_by_permutes(x, axis, dim):
    count = lax.axis_size(axis)
    me = lax.axis_index(axis)
    pieces = [x] + [
        lax.ppermute(x, axis, [(i, (i + shift) % count) for i in range(count)])
        for shift in range(1, count)
    ]
    stacked = jnp.stack(pieces[::-1], axis=0)
    ordered = jnp.roll(stacked, me + 1, axis=0)
    ordered = jnp.moveaxis(ordered, 0, dim)
    shape = list(x.shape)
    shape[dim] *= count
    return ordered.reshape(shape)


def rotate(vectors, position):
    half_dim = vectors.shape[-1] // 2
    frequency = rope_theta ** (-(jnp.arange(half_dim, dtype=jnp.float32) / half_dim))
    angles = position.astype(jnp.float32)[:, None, None] * frequency[None, None, :]
    cosine = jnp.cos(angles)
    sine_part = jnp.sin(angles)
    first_half = vectors[..., :half_dim]
    second = vectors[..., half_dim:]
    return jnp.concatenate(
        [first_half * cosine - second * sine_part, second * cosine + first_half * sine_part],
        axis=-1,
    )


def normalize(group_rows, attn_gain):
    features = group_rows.astype(jnp.float32)
    root_mean = jnp.sqrt(jnp.mean(features * features, axis=-1, keepdims=True) + norm_eps)
    return (features / root_mean * attn_gain).astype(jnp.bfloat16)


def token_positions(token_request, group_lengths, request_count):
    member = (token_request[:, None] == jnp.arange(request_count, dtype=jnp.int32)[None, :]).astype(
        jnp.int32
    )
    earlier = jnp.sum((jnp.cumsum(member, axis=0) - member) * member, axis=1)
    return jnp.sum(member * group_lengths[None, :], axis=1) + earlier


def build_mask(token_request, group_lengths, max_len):
    request_count = group_lengths.shape[0]
    key_index = jnp.arange(request_count * max_len, dtype=jnp.int32)
    key_request = key_index // max_len
    key_alive = key_index % max_len < group_lengths[key_request]
    cached = (token_request[:, None] == key_request[None, :]) & key_alive[None, :]
    token_order = jnp.arange(token_request.shape[0], dtype=jnp.int32)
    fresh = (token_request[:, None] == token_request[None, :]) & (
        token_order[None, :] <= token_order[:, None]
    )
    return jnp.concatenate([cached, fresh], axis=1)


def weigh(scores, allowed):
    masked = jnp.where(allowed, scores, -1e30)
    row_top = jnp.max(masked, axis=-1, keepdims=True)
    exponent = jnp.exp(masked - row_top)
    return (exponent / jnp.sum(exponent, axis=-1, keepdims=True)).astype(jnp.bfloat16)


def on_device(
    tokens, attn_gain, q_weight, k_weight, v_weight, kv_pool, page_table, lengths, token_request
):
    groups = lax.axis_size(GROUP)
    group_idx = lax.axis_index(GROUP)
    mp_idx = lax.axis_index("mp")
    pool_pages = kv_pool.shape[0]
    pair_count = kv_pool.shape[1]
    page_len = kv_pool.shape[3]
    head_dim = kv_pool.shape[4]
    requests_here = lengths.shape[0]
    slot_count = pool_pages // requests_here
    max_len = slot_count * page_len
    capacity = 2 * pool_pages // groups
    flat_table = page_table.reshape(-1)
    slot_ids = jnp.arange(flat_table.shape[0], dtype=jnp.int32)
    owner_slot = jnp.zeros((flat_table.shape[0],), jnp.int32).at[flat_table].set(slot_ids)
    held_slots = lax.dynamic_slice_in_dim(owner_slot, group_idx * pool_pages, pool_pages)
    target_owner = held_slots // pool_pages
    slot_local = held_slots % pool_pages
    owner_hits = (target_owner[:, None] == jnp.arange(groups, dtype=jnp.int32)[None, :]).astype(
        jnp.int32
    )
    order_within = jnp.sum((jnp.cumsum(owner_hits, axis=0) - owner_hits) * owner_hits, axis=1)
    buffer_row = target_owner * capacity + order_within
    page_rows = kv_pool.reshape(pool_pages, -1)
    row_width = page_rows.shape[1]
    outgoing = (
        jnp.zeros((groups * capacity, row_width), jnp.bfloat16)
        .at[buffer_row]
        .set(page_rows)
        .reshape(groups, capacity, row_width)
    )
    outgoing_slots = (
        jnp.full((groups * capacity,), -1, jnp.int32)
        .at[buffer_row]
        .set(slot_local)
        .reshape(groups, capacity)
    )
    arrived, arrived_slots = (
        lax.all_to_all(outgoing, GROUP, split_axis=0, concat_axis=0, tiled=True),
        lax.all_to_all(outgoing_slots, GROUP, split_axis=0, concat_axis=0, tiled=True),
    )
    landing = jnp.where(arrived_slots < 0, pool_pages, arrived_slots).reshape(-1)
    placed = (
        jnp.zeros((pool_pages + 1, row_width), jnp.bfloat16)
        .at[landing]
        .set(arrived.reshape(-1, row_width))[:pool_pages]
    )
    decoded = placed.reshape(requests_here, slot_count, pair_count, 2, page_len, head_dim)
    decoded = decoded.transpose(0, 2, 3, 1, 4, 5).reshape(
        requests_here, pair_count, 2, max_len, head_dim
    )
    alive_mask = jnp.arange(max_len, dtype=jnp.int32)[None, :] < lengths[:, None]
    decoded = jnp.where(alive_mask[:, None, None, :, None], decoded, jnp.zeros((), jnp.bfloat16))
    whole_rows = gather_by_permutes(tokens, "mp", 1)
    normed = normalize(whole_rows, attn_gain)
    rows_here = tokens.shape[0]
    heads_here = q_weight.shape[1] // head_dim
    per_kv = HEADS // KVH
    first_kv = mp_idx * heads_here // per_kv
    is_even = mp_idx % 2 == 0
    kv_weight = jnp.concatenate([k_weight, v_weight], axis=1)
    own_kv_cols = lax.dynamic_slice_in_dim(
        kv_weight, (mp_idx % 2) * k_weight.shape[1] + first_kv * head_dim, head_dim, 1
    )
    q_cols = q_weight.shape[1]
    joined_cols = jnp.concatenate([q_weight, own_kv_cols], axis=1)
    joined_sum = jnp.dot(
        normed,
        lax.all_gather(gather_by_permutes(joined_cols, "gy", 0), "gz", axis=0, tiled=True),
        preferred_element_type=jnp.float32,
    )
    query_sum = joined_sum[:, :q_cols]
    kv_sum = joined_sum[:, q_cols:]
    position = token_positions(token_request, lengths, requests_here)
    queries = (
        rotate(query_sum.reshape(rows_here, heads_here, head_dim), position)
        .astype(jnp.bfloat16)
        .transpose(1, 0, 2)
    )
    rotated_kv = rotate(kv_sum.reshape(rows_here, 1, head_dim), position)[:, 0]
    own_kv = jnp.where(is_even, rotated_kv, kv_sum).astype(jnp.bfloat16)
    other_kv = from_partner(own_kv, "mp", 0)
    new_keys = jnp.where(is_even, own_kv, other_kv)
    new_values = jnp.where(is_even, other_kv, own_kv)
    allowed = build_mask(token_request, lengths, max_len)
    score_scale = head_dim ** (-0.5)
    partner_cache = from_partner(decoded, "mp", 0)
    layer_zero = jnp.where(is_even, decoded, partner_cache)[:, 0]
    all_keys = jnp.concatenate(
        [layer_zero[:, 0].reshape(requests_here * max_len, head_dim), new_keys], axis=0
    )
    all_values = jnp.concatenate(
        [layer_zero[:, 1].reshape(requests_here * max_len, head_dim), new_values], axis=0
    )

    def attend(query_one):
        scores = (
            jnp.einsum("td,nd->tn", query_one, all_keys, preferred_element_type=jnp.float32)
            * score_scale
        )
        attn_probs = weigh(scores, allowed)
        return jnp.dot(attn_probs, all_values, preferred_element_type=jnp.float32).astype(
            jnp.bfloat16
        )

    heads_out = lax.map(attend, queries)
    attention = heads_out.transpose(1, 0, 2).reshape(rows_here, heads_here * head_dim)
    return (attention, partner_cache)


def split_mesh(mesh):
    devices = mesh.devices
    groups, parts = devices.shape
    try:
        z_of = [d.coords[2] for d in devices[:, 0]]
        inner = next((i for i in range(1, groups) if z_of[i] != z_of[0]), groups)
    except (AttributeError, IndexError, TypeError):
        inner = int(round(groups**0.5))
    return Mesh(devices.reshape(groups // inner, inner, parts), ("gz", "gy", "mp"))


def solution(mesh):
    return jax.shard_map(
        on_device,
        mesh=split_mesh(mesh),
        in_specs=(
            P(GROUP, "mp"),
            P(),
            P(GROUP, "mp"),
            P(GROUP, None),
            P(GROUP, None),
            P(GROUP, "mp", None, None, None),
            P(),
            P(GROUP),
            P(GROUP),
        ),
        out_specs=(P(GROUP, "mp"), P(GROUP, "mp", None, None, None)),
        check_vma=False,
    )
```

```python
import jax
import jax.numpy as jnp
from jax import lax
from jax.sharding import Mesh, PartitionSpec as P

HEADS = 32
KVH = 4
GROUP = ("gz", "gy")


rope_theta = 5000000.0
norm_eps = 1e-05


def from_partner(x, axis, bit):
    return lax.ppermute(x, axis, [(i, i ^ 1 << bit) for i in range(lax.axis_size(axis))])


def gather_by_all_to_all(x, axis, dim):
    count = lax.axis_size(axis)
    spread = jnp.broadcast_to(x[None], (count,) + x.shape)
    ordered = lax.all_to_all(spread, axis, 0, 0, tiled=True)
    ordered = jnp.moveaxis(ordered, 0, dim)
    shape = list(x.shape)
    shape[dim] *= count
    return ordered.reshape(shape)


def rotate(vectors, position):
    half_dim = vectors.shape[-1] // 2
    frequency = rope_theta ** (-(jnp.arange(half_dim, dtype=jnp.float32) / half_dim))
    angles = position.astype(jnp.float32)[:, None, None] * frequency[None, None, :]
    cosine = jnp.cos(angles)
    sine_part = jnp.sin(angles)
    first_half = vectors[..., :half_dim]
    second = vectors[..., half_dim:]
    return jnp.concatenate(
        [first_half * cosine - second * sine_part, second * cosine + first_half * sine_part],
        axis=-1,
    )


def normalize(group_rows, attn_gain):
    features = group_rows.astype(jnp.float32)
    root_mean = jnp.sqrt(jnp.mean(features * features, axis=-1, keepdims=True) + norm_eps)
    return (features / root_mean * attn_gain).astype(jnp.bfloat16)


def token_positions(token_request, group_lengths, request_count):
    member = (token_request[:, None] == jnp.arange(request_count, dtype=jnp.int32)[None, :]).astype(
        jnp.int32
    )
    earlier = jnp.sum((jnp.cumsum(member, axis=0) - member) * member, axis=1)
    return jnp.sum(member * group_lengths[None, :], axis=1) + earlier


def build_mask(token_request, group_lengths, max_len):
    request_count = group_lengths.shape[0]
    key_index = jnp.arange(request_count * max_len, dtype=jnp.int32)
    key_request = key_index // max_len
    key_alive = key_index % max_len < group_lengths[key_request]
    cached = (token_request[:, None] == key_request[None, :]) & key_alive[None, :]
    token_order = jnp.arange(token_request.shape[0], dtype=jnp.int32)
    fresh = (token_request[:, None] == token_request[None, :]) & (
        token_order[None, :] <= token_order[:, None]
    )
    return jnp.concatenate([cached, fresh], axis=1)


def weigh(scores, allowed):
    masked = jnp.where(allowed, scores, -1e30)
    row_top = jnp.max(masked, axis=-1, keepdims=True)
    exponent = jnp.exp(masked - row_top)
    return (exponent / jnp.sum(exponent, axis=-1, keepdims=True)).astype(jnp.bfloat16)


def on_device(
    tokens, attn_gain, q_weight, k_weight, v_weight, kv_pool, page_table, lengths, token_request
):
    groups = lax.axis_size(GROUP)
    group_idx = lax.axis_index(GROUP)
    mp_idx = lax.axis_index("mp")
    pool_pages = kv_pool.shape[0]
    pair_count = kv_pool.shape[1]
    page_len = kv_pool.shape[3]
    head_dim = kv_pool.shape[4]
    requests_here = lengths.shape[0]
    slot_count = pool_pages // requests_here
    max_len = slot_count * page_len
    capacity = 2 * pool_pages // groups
    flat_table = page_table.reshape(-1)
    slot_ids = jnp.arange(flat_table.shape[0], dtype=jnp.int32)
    held_pages = group_idx * pool_pages + jnp.arange(pool_pages, dtype=jnp.int32)
    held_slots = jnp.sum(
        jnp.where(flat_table[None, :] == held_pages[:, None], slot_ids[None, :], 0), axis=1
    )
    target_owner = held_slots // pool_pages
    owner_hits = (target_owner[:, None] == jnp.arange(groups, dtype=jnp.int32)[None, :]).astype(
        jnp.int32
    )
    order_within = jnp.sum((jnp.cumsum(owner_hits, axis=0) - owner_hits) * owner_hits, axis=1)
    buffer_row = target_owner * capacity + order_within
    page_rows = kv_pool.reshape(pool_pages, -1)
    row_width = page_rows.shape[1]
    buffer_ids = jnp.arange(groups * capacity, dtype=jnp.int32)
    send_pick = (buffer_ids[:, None] == buffer_row[None, :]).astype(jnp.bfloat16)
    outgoing = (
        jnp.dot(send_pick, page_rows, preferred_element_type=jnp.float32)
        .astype(jnp.bfloat16)
        .reshape(groups, capacity, row_width)
    )
    arrived = lax.all_to_all(outgoing, GROUP, split_axis=0, concat_axis=0, tiled=True)
    my_pages = lax.dynamic_slice_in_dim(flat_table, group_idx * pool_pages, pool_pages)
    sender = my_pages // pool_pages
    earlier_same = (sender[None, :] == sender[:, None]) & (my_pages[None, :] < my_pages[:, None])
    arrival_row = sender * capacity + jnp.sum(earlier_same.astype(jnp.int32), axis=1)
    take_pick = (arrival_row[:, None] == buffer_ids[None, :]).astype(jnp.bfloat16)
    placed = jnp.dot(
        take_pick, arrived.reshape(-1, row_width), preferred_element_type=jnp.float32
    ).astype(jnp.bfloat16)
    decoded = placed.reshape(requests_here, slot_count, pair_count, 2, page_len, head_dim)
    decoded = decoded.transpose(0, 2, 3, 1, 4, 5).reshape(
        requests_here, pair_count, 2, max_len, head_dim
    )
    alive_mask = jnp.arange(max_len, dtype=jnp.int32)[None, :] < lengths[:, None]
    decoded = jnp.where(alive_mask[:, None, None, :, None], decoded, jnp.zeros((), jnp.bfloat16))
    whole_rows = gather_by_all_to_all(tokens, "mp", 1)
    normed = normalize(whole_rows, attn_gain)
    rows_here = tokens.shape[0]
    heads_here = q_weight.shape[1] // head_dim
    per_kv = HEADS // KVH
    first_kv = mp_idx * heads_here // per_kv
    is_even = mp_idx % 2 == 0
    kv_weight = jnp.concatenate([k_weight, v_weight], axis=1)
    own_kv_cols = lax.dynamic_slice_in_dim(
        kv_weight, (mp_idx % 2) * k_weight.shape[1] + first_kv * head_dim, head_dim, 1
    )
    q_cols = q_weight.shape[1]
    joined_cols = jnp.concatenate([q_weight, own_kv_cols], axis=1)
    joined_sum = jnp.dot(
        normed,
        lax.all_gather(joined_cols, GROUP, axis=0, tiled=True),
        preferred_element_type=jnp.float32,
    )
    query_sum = joined_sum[:, :q_cols]
    kv_sum = joined_sum[:, q_cols:]
    position = token_positions(token_request, lengths, requests_here)
    queries = (
        rotate(query_sum.reshape(rows_here, heads_here, head_dim), position)
        .astype(jnp.bfloat16)
        .transpose(1, 0, 2)
    )
    rotated_kv = rotate(kv_sum.reshape(rows_here, 1, head_dim), position)[:, 0]
    own_kv = jnp.where(is_even, rotated_kv, kv_sum).astype(jnp.bfloat16)
    other_kv = from_partner(own_kv, "mp", 0)
    new_keys = jnp.where(is_even, own_kv, other_kv)
    new_values = jnp.where(is_even, other_kv, own_kv)
    allowed = build_mask(token_request, lengths, max_len)
    score_scale = head_dim ** (-0.5)
    partner_cache = from_partner(decoded, "mp", 0)
    layer_zero = jnp.where(is_even, decoded, partner_cache)[:, 0]
    all_keys = jnp.concatenate(
        [layer_zero[:, 0].reshape(requests_here * max_len, head_dim), new_keys], axis=0
    )
    all_values = jnp.concatenate(
        [layer_zero[:, 1].reshape(requests_here * max_len, head_dim), new_values], axis=0
    )

    def attend(query_one):
        scores = (
            jnp.einsum("td,nd->tn", query_one, all_keys, preferred_element_type=jnp.float32)
            * score_scale
        )
        attn_probs = weigh(scores, allowed)
        return jnp.dot(attn_probs, all_values, preferred_element_type=jnp.float32).astype(
            jnp.bfloat16
        )

    heads_out = lax.map(attend, queries)
    attention = heads_out.transpose(1, 0, 2).reshape(rows_here, heads_here * head_dim)
    return (attention, partner_cache)


def split_mesh(mesh):
    devices = mesh.devices
    groups, parts = devices.shape
    try:
        z_of = [d.coords[2] for d in devices[:, 0]]
        inner = next((i for i in range(1, groups) if z_of[i] != z_of[0]), groups)
    except (AttributeError, IndexError, TypeError):
        inner = int(round(groups**0.5))
    return Mesh(devices.reshape(groups // inner, inner, parts), ("gz", "gy", "mp"))


def solution(mesh):
    return jax.shard_map(
        on_device,
        mesh=split_mesh(mesh),
        in_specs=(
            P(GROUP, "mp"),
            P(),
            P(GROUP, "mp"),
            P(GROUP, None),
            P(GROUP, None),
            P(GROUP, "mp", None, None, None),
            P(),
            P(GROUP),
            P(GROUP),
        ),
        out_specs=(P(GROUP, "mp"), P(GROUP, "mp", None, None, None)),
        check_vma=False,
    )
```

```python
import jax
import jax.numpy as jnp
from jax import lax
from jax.sharding import Mesh, PartitionSpec as P

HEADS = 32
KVH = 4
GROUP = ("gz", "gy")


rope_theta = 5000000.0
norm_eps = 1e-05


def from_partner(x, axis, bit):
    return lax.ppermute(x, axis, [(i, i ^ 1 << bit) for i in range(lax.axis_size(axis))])


def gather_by_all_to_all(x, axis, dim):
    count = lax.axis_size(axis)
    spread = jnp.broadcast_to(x[None], (count,) + x.shape)
    ordered = lax.all_to_all(spread, axis, 0, 0, tiled=True)
    ordered = jnp.moveaxis(ordered, 0, dim)
    shape = list(x.shape)
    shape[dim] *= count
    return ordered.reshape(shape)


def rotate(vectors, position):
    half_dim = vectors.shape[-1] // 2
    frequency = rope_theta ** (-(jnp.arange(half_dim, dtype=jnp.float32) / half_dim))
    angles = position.astype(jnp.float32)[:, None, None] * frequency[None, None, :]
    cosine = jnp.cos(angles)
    sine_part = jnp.sin(angles)
    first_half = vectors[..., :half_dim]
    second = vectors[..., half_dim:]
    return jnp.concatenate(
        [first_half * cosine - second * sine_part, second * cosine + first_half * sine_part],
        axis=-1,
    )


def normalize(group_rows, attn_gain):
    features = group_rows.astype(jnp.float32)
    root_mean = jnp.sqrt(jnp.mean(features * features, axis=-1, keepdims=True) + norm_eps)
    return (features / root_mean * attn_gain).astype(jnp.bfloat16)


def token_positions(token_request, group_lengths, request_count):
    member = (token_request[:, None] == jnp.arange(request_count, dtype=jnp.int32)[None, :]).astype(
        jnp.int32
    )
    earlier = jnp.sum((jnp.cumsum(member, axis=0) - member) * member, axis=1)
    return jnp.sum(member * group_lengths[None, :], axis=1) + earlier


def build_mask(token_request, group_lengths, max_len):
    request_count = group_lengths.shape[0]
    key_index = jnp.arange(request_count * max_len, dtype=jnp.int32)
    key_request = key_index // max_len
    key_alive = key_index % max_len < group_lengths[key_request]
    cached = (token_request[:, None] == key_request[None, :]) & key_alive[None, :]
    token_order = jnp.arange(token_request.shape[0], dtype=jnp.int32)
    fresh = (token_request[:, None] == token_request[None, :]) & (
        token_order[None, :] <= token_order[:, None]
    )
    return jnp.concatenate([cached, fresh], axis=1)


def weigh(scores, allowed):
    masked = jnp.where(allowed, scores, -1e30)
    row_top = jnp.max(masked, axis=-1, keepdims=True)
    exponent = jnp.exp(masked - row_top)
    return (exponent / jnp.sum(exponent, axis=-1, keepdims=True)).astype(jnp.bfloat16)


def on_device(
    tokens, attn_gain, q_weight, k_weight, v_weight, kv_pool, page_table, lengths, token_request
):
    groups = lax.axis_size(GROUP)
    group_idx = lax.axis_index(GROUP)
    mp_idx = lax.axis_index("mp")
    pool_pages = kv_pool.shape[0]
    pair_count = kv_pool.shape[1]
    page_len = kv_pool.shape[3]
    head_dim = kv_pool.shape[4]
    requests_here = lengths.shape[0]
    slot_count = pool_pages // requests_here
    max_len = slot_count * page_len
    capacity = 2 * pool_pages // groups
    flat_table = page_table.reshape(-1)
    slot_ids = jnp.arange(flat_table.shape[0], dtype=jnp.int32)
    held_pages = group_idx * pool_pages + jnp.arange(pool_pages, dtype=jnp.int32)
    held_slots = jnp.sum(
        jnp.where(flat_table[None, :] == held_pages[:, None], slot_ids[None, :], 0), axis=1
    )
    target_owner = held_slots // pool_pages
    owner_hits = (target_owner[:, None] == jnp.arange(groups, dtype=jnp.int32)[None, :]).astype(
        jnp.int32
    )
    order_within = jnp.sum((jnp.cumsum(owner_hits, axis=0) - owner_hits) * owner_hits, axis=1)
    buffer_row = target_owner * capacity + order_within
    page_rows = kv_pool.reshape(pool_pages, -1)
    row_width = page_rows.shape[1]
    buffer_ids = jnp.arange(groups * capacity, dtype=jnp.int32)
    send_pick = (buffer_ids[:, None] == buffer_row[None, :]).astype(jnp.bfloat16)
    outgoing = (
        jnp.dot(send_pick, page_rows, preferred_element_type=jnp.float32)
        .astype(jnp.bfloat16)
        .reshape(groups, capacity, row_width)
    )
    arrived = lax.all_to_all(outgoing, GROUP, split_axis=0, concat_axis=0, tiled=True)
    my_pages = lax.dynamic_slice_in_dim(flat_table, group_idx * pool_pages, pool_pages)
    sender = my_pages // pool_pages
    earlier_same = (sender[None, :] == sender[:, None]) & (my_pages[None, :] < my_pages[:, None])
    arrival_row = sender * capacity + jnp.sum(earlier_same.astype(jnp.int32), axis=1)
    take_pick = (arrival_row[:, None] == buffer_ids[None, :]).astype(jnp.bfloat16)
    placed = jnp.dot(
        take_pick, arrived.reshape(-1, row_width), preferred_element_type=jnp.float32
    ).astype(jnp.bfloat16)
    decoded = placed.reshape(requests_here, slot_count, pair_count, 2, page_len, head_dim)
    decoded = decoded.transpose(0, 2, 3, 1, 4, 5).reshape(
        requests_here, pair_count, 2, max_len, head_dim
    )
    alive_mask = jnp.arange(max_len, dtype=jnp.int32)[None, :] < lengths[:, None]
    decoded = jnp.where(alive_mask[:, None, None, :, None], decoded, jnp.zeros((), jnp.bfloat16))
    whole_rows = gather_by_all_to_all(tokens, "mp", 1)
    normed = normalize(whole_rows, attn_gain)
    rows_here = tokens.shape[0]
    heads_here = q_weight.shape[1] // head_dim
    per_kv = HEADS // KVH
    first_kv = mp_idx * heads_here // per_kv
    is_even = mp_idx % 2 == 0
    kv_weight = jnp.concatenate([k_weight, v_weight], axis=1)
    own_kv_cols = lax.dynamic_slice_in_dim(
        kv_weight, (mp_idx % 2) * k_weight.shape[1] + first_kv * head_dim, head_dim, 1
    )
    q_cols = q_weight.shape[1]
    joined_cols = jnp.concatenate([q_weight, own_kv_cols], axis=1)
    joined_sum = jnp.dot(
        normed,
        lax.all_gather(joined_cols, GROUP, axis=0, tiled=True),
        preferred_element_type=jnp.float32,
    )
    query_sum = joined_sum[:, :q_cols]
    kv_sum = joined_sum[:, q_cols:]
    position = token_positions(token_request, lengths, requests_here)
    queries = rotate(query_sum.reshape(rows_here, heads_here, head_dim), position).astype(
        jnp.bfloat16
    )
    rotated_kv = rotate(kv_sum.reshape(rows_here, 1, head_dim), position)[:, 0]
    own_kv = jnp.where(is_even, rotated_kv, kv_sum).astype(jnp.bfloat16)
    other_kv = from_partner(own_kv, "mp", 0)
    new_keys = jnp.where(is_even, own_kv, other_kv)
    new_values = jnp.where(is_even, other_kv, own_kv)
    allowed = build_mask(token_request, lengths, max_len)
    score_scale = head_dim ** (-0.5)
    partner_cache = from_partner(decoded, "mp", 0)
    layer_zero = jnp.where(is_even, decoded, partner_cache)[:, 0]
    all_keys = jnp.concatenate(
        [layer_zero[:, 0].reshape(requests_here * max_len, head_dim), new_keys], axis=0
    )
    all_values = jnp.concatenate(
        [layer_zero[:, 1].reshape(requests_here * max_len, head_dim), new_values], axis=0
    )

    scores = (
        jnp.einsum("thd,nd->thn", queries, all_keys, preferred_element_type=jnp.float32)
        * score_scale
    )
    attn_probs = weigh(scores, allowed[:, None, :])
    heads_out = jnp.einsum(
        "thn,nd->thd", attn_probs, all_values, preferred_element_type=jnp.float32
    ).astype(jnp.bfloat16)
    attention = heads_out.reshape(rows_here, heads_here * head_dim)
    return (attention, partner_cache)


def split_mesh(mesh):
    devices = mesh.devices
    groups, parts = devices.shape
    try:
        z_of = [d.coords[2] for d in devices[:, 0]]
        inner = next((i for i in range(1, groups) if z_of[i] != z_of[0]), groups)
    except (AttributeError, IndexError, TypeError):
        inner = int(round(groups**0.5))
    return Mesh(devices.reshape(groups // inner, inner, parts), ("gz", "gy", "mp"))


def solution(mesh):
    return jax.shard_map(
        on_device,
        mesh=split_mesh(mesh),
        in_specs=(
            P(GROUP, "mp"),
            P(),
            P(GROUP, "mp"),
            P(GROUP, None),
            P(GROUP, None),
            P(GROUP, "mp", None, None, None),
            P(),
            P(GROUP),
            P(GROUP),
        ),
        out_specs=(P(GROUP, "mp"), P(GROUP, "mp", None, None, None)),
        check_vma=False,
    )
```

```python
import jax
import jax.numpy as jnp
from jax import lax
from jax.sharding import Mesh, PartitionSpec as P

HEADS = 32
KVH = 4
GROUP = ("gz", "gy")


rope_theta = 5000000.0
norm_eps = 1e-05


def from_partner(x, axis, bit):
    return lax.ppermute(x, axis, [(i, i ^ 1 << bit) for i in range(lax.axis_size(axis))])


def gather_by_all_to_all(x, axis, dim):
    count = lax.axis_size(axis)
    spread = jnp.broadcast_to(x[None], (count,) + x.shape)
    ordered = lax.all_to_all(spread, axis, 0, 0, tiled=True)
    ordered = jnp.moveaxis(ordered, 0, dim)
    shape = list(x.shape)
    shape[dim] *= count
    return ordered.reshape(shape)


def rotate(vectors, position):
    half_dim = vectors.shape[-1] // 2
    frequency = rope_theta ** (-(jnp.arange(half_dim, dtype=jnp.float32) / half_dim))
    angles = position.astype(jnp.float32)[:, None, None] * frequency[None, None, :]
    cosine = jnp.cos(angles)
    sine_part = jnp.sin(angles)
    first_half = vectors[..., :half_dim]
    second = vectors[..., half_dim:]
    return jnp.concatenate(
        [first_half * cosine - second * sine_part, second * cosine + first_half * sine_part],
        axis=-1,
    )


def normalize(group_rows, attn_gain):
    features = group_rows.astype(jnp.float32)
    root_mean = jnp.sqrt(jnp.mean(features * features, axis=-1, keepdims=True) + norm_eps)
    return (features / root_mean * attn_gain).astype(jnp.bfloat16)


def token_positions(token_request, group_lengths, request_count):
    member = (token_request[:, None] == jnp.arange(request_count, dtype=jnp.int32)[None, :]).astype(
        jnp.int32
    )
    earlier = jnp.sum((jnp.cumsum(member, axis=0) - member) * member, axis=1)
    return jnp.sum(member * group_lengths[None, :], axis=1) + earlier


def build_mask(token_request, group_lengths, max_len):
    request_count = group_lengths.shape[0]
    key_index = jnp.arange(request_count * max_len, dtype=jnp.int32)
    key_request = key_index // max_len
    key_alive = key_index % max_len < group_lengths[key_request]
    cached = (token_request[:, None] == key_request[None, :]) & key_alive[None, :]
    token_order = jnp.arange(token_request.shape[0], dtype=jnp.int32)
    fresh = (token_request[:, None] == token_request[None, :]) & (
        token_order[None, :] <= token_order[:, None]
    )
    return jnp.concatenate([cached, fresh], axis=1)


def weigh(scores, allowed):
    masked = jnp.where(allowed, scores, -1e30)
    row_top = jnp.max(masked, axis=-1, keepdims=True)
    exponent = jnp.exp(masked - row_top)
    return (exponent / jnp.sum(exponent, axis=-1, keepdims=True)).astype(jnp.bfloat16)


def on_device(
    tokens, attn_gain, q_weight, k_weight, v_weight, kv_pool, page_table, lengths, token_request
):
    groups = lax.axis_size(GROUP)
    group_idx = lax.axis_index(GROUP)
    mp_idx = lax.axis_index("mp")
    pool_pages = kv_pool.shape[0]
    pair_count = kv_pool.shape[1]
    page_len = kv_pool.shape[3]
    head_dim = kv_pool.shape[4]
    requests_here = lengths.shape[0]
    slot_count = pool_pages // requests_here
    max_len = slot_count * page_len
    capacity = 2 * pool_pages // groups
    flat_table = page_table.reshape(-1)
    slot_ids = jnp.arange(flat_table.shape[0], dtype=jnp.int32)
    held_pages = group_idx * pool_pages + jnp.arange(pool_pages, dtype=jnp.int32)
    held_slots = jnp.sum(
        jnp.where(flat_table[None, :] == held_pages[:, None], slot_ids[None, :], 0), axis=1
    )
    target_owner = held_slots // pool_pages
    owner_hits = (target_owner[:, None] == jnp.arange(groups, dtype=jnp.int32)[None, :]).astype(
        jnp.int32
    )
    order_within = jnp.sum((jnp.cumsum(owner_hits, axis=0) - owner_hits) * owner_hits, axis=1)
    buffer_row = target_owner * capacity + order_within
    page_rows = kv_pool.reshape(pool_pages, -1)
    row_width = page_rows.shape[1]
    buffer_ids = jnp.arange(groups * capacity, dtype=jnp.int32)
    send_pick = (buffer_ids[:, None] == buffer_row[None, :]).astype(jnp.bfloat16)
    outgoing = (
        jnp.dot(send_pick, page_rows, preferred_element_type=jnp.float32)
        .astype(jnp.bfloat16)
        .reshape(groups, capacity, row_width)
    )
    arrived = lax.all_to_all(outgoing, GROUP, split_axis=0, concat_axis=0, tiled=True)
    my_pages = lax.dynamic_slice_in_dim(flat_table, group_idx * pool_pages, pool_pages)
    sender = my_pages // pool_pages
    earlier_same = (sender[None, :] == sender[:, None]) & (my_pages[None, :] < my_pages[:, None])
    arrival_row = sender * capacity + jnp.sum(earlier_same.astype(jnp.int32), axis=1)
    take_pick = (arrival_row[:, None] == buffer_ids[None, :]).astype(jnp.bfloat16)
    placed = jnp.dot(
        take_pick, arrived.reshape(-1, row_width), preferred_element_type=jnp.float32
    ).astype(jnp.bfloat16)
    decoded = placed.reshape(requests_here, slot_count, pair_count, 2, page_len, head_dim)
    decoded = decoded.transpose(0, 2, 3, 1, 4, 5).reshape(
        requests_here, pair_count, 2, max_len, head_dim
    )
    alive_mask = jnp.arange(max_len, dtype=jnp.int32)[None, :] < lengths[:, None]
    decoded = jnp.where(alive_mask[:, None, None, :, None], decoded, jnp.zeros((), jnp.bfloat16))
    whole_rows = gather_by_all_to_all(tokens, "mp", 1)
    normed = normalize(whole_rows, attn_gain)
    rows_here = tokens.shape[0]
    heads_here = q_weight.shape[1] // head_dim
    per_kv = HEADS // KVH
    first_kv = mp_idx * heads_here // per_kv
    is_even = mp_idx % 2 == 0
    kv_weight = jnp.concatenate([k_weight, v_weight], axis=1)
    own_kv_cols = lax.dynamic_slice_in_dim(
        kv_weight, (mp_idx % 2) * k_weight.shape[1] + first_kv * head_dim, head_dim, 1
    )
    q_cols = q_weight.shape[1]
    joined_cols = jnp.concatenate([q_weight, own_kv_cols], axis=1)
    near_rows = lax.all_gather(joined_cols, "gy", axis=0, tiled=True)
    far = lax.axis_size("gz")
    feature_blocks = normed.reshape(rows_here, far, near_rows.shape[0]).transpose(1, 0, 2)
    arrived_rows = lax.all_to_all(feature_blocks, "gz", 0, 0, tiled=True)
    partial_sums = jnp.einsum(
        "ztf,fc->ztc", arrived_rows, near_rows, preferred_element_type=jnp.float32
    )
    joined_sum = lax.psum_scatter(partial_sums, "gz", scatter_dimension=0, tiled=True)[0]
    query_sum = joined_sum[:, :q_cols]
    kv_sum = joined_sum[:, q_cols:]
    position = token_positions(token_request, lengths, requests_here)
    queries = rotate(query_sum.reshape(rows_here, heads_here, head_dim), position).astype(
        jnp.bfloat16
    )
    rotated_kv = rotate(kv_sum.reshape(rows_here, 1, head_dim), position)[:, 0]
    own_kv = jnp.where(is_even, rotated_kv, kv_sum).astype(jnp.bfloat16)
    other_kv = from_partner(own_kv, "mp", 0)
    new_keys = jnp.where(is_even, own_kv, other_kv)
    new_values = jnp.where(is_even, other_kv, own_kv)
    allowed = build_mask(token_request, lengths, max_len)
    score_scale = head_dim ** (-0.5)
    partner_cache = from_partner(decoded, "mp", 0)
    layer_zero = jnp.where(is_even, decoded, partner_cache)[:, 0]
    all_keys = jnp.concatenate(
        [layer_zero[:, 0].reshape(requests_here * max_len, head_dim), new_keys], axis=0
    )
    all_values = jnp.concatenate(
        [layer_zero[:, 1].reshape(requests_here * max_len, head_dim), new_values], axis=0
    )

    scores = (
        jnp.einsum("thd,nd->thn", queries, all_keys, preferred_element_type=jnp.float32)
        * score_scale
    )
    attn_probs = weigh(scores, allowed[:, None, :])
    heads_out = jnp.einsum(
        "thn,nd->thd", attn_probs, all_values, preferred_element_type=jnp.float32
    ).astype(jnp.bfloat16)
    attention = heads_out.reshape(rows_here, heads_here * head_dim)
    return (attention, partner_cache)


def split_mesh(mesh):
    devices = mesh.devices
    groups, parts = devices.shape
    try:
        z_of = [d.coords[2] for d in devices[:, 0]]
        inner = next((i for i in range(1, groups) if z_of[i] != z_of[0]), groups)
    except (AttributeError, IndexError, TypeError):
        inner = int(round(groups**0.5))
    return Mesh(devices.reshape(groups // inner, inner, parts), ("gz", "gy", "mp"))


def solution(mesh):
    return jax.shard_map(
        on_device,
        mesh=split_mesh(mesh),
        in_specs=(
            P(GROUP, "mp"),
            P(),
            P(GROUP, "mp"),
            P(GROUP, None),
            P(GROUP, None),
            P(GROUP, "mp", None, None, None),
            P(),
            P(GROUP),
            P(GROUP),
        ),
        out_specs=(P(GROUP, "mp"), P(GROUP, "mp", None, None, None)),
        check_vma=False,
    )
```

```python
import jax
import jax.numpy as jnp
from jax import lax
from jax.sharding import Mesh, PartitionSpec as P

HEADS = 32
KVH = 4
GROUP = ("gz", "gy")


rope_theta = 5000000.0
norm_eps = 1e-05


def from_partner(x, axis, bit):
    return lax.ppermute(x, axis, [(i, i ^ 1 << bit) for i in range(lax.axis_size(axis))])


def gather_by_all_to_all(x, axis, dim):
    count = lax.axis_size(axis)
    spread = jnp.broadcast_to(x[None], (count,) + x.shape)
    ordered = lax.all_to_all(spread, axis, 0, 0, tiled=True)
    ordered = jnp.moveaxis(ordered, 0, dim)
    shape = list(x.shape)
    shape[dim] *= count
    return ordered.reshape(shape)


def rotate(vectors, position):
    half_dim = vectors.shape[-1] // 2
    frequency = rope_theta ** (-(jnp.arange(half_dim, dtype=jnp.float32) / half_dim))
    angles = position.astype(jnp.float32)[:, None, None] * frequency[None, None, :]
    cosine = jnp.cos(angles)
    sine_part = jnp.sin(angles)
    first_half = vectors[..., :half_dim]
    second = vectors[..., half_dim:]
    return jnp.concatenate(
        [first_half * cosine - second * sine_part, second * cosine + first_half * sine_part],
        axis=-1,
    )


def normalize(group_rows, attn_gain):
    features = group_rows.astype(jnp.float32)
    root_mean = jnp.sqrt(jnp.mean(features * features, axis=-1, keepdims=True) + norm_eps)
    return (features / root_mean * attn_gain).astype(jnp.bfloat16)


def token_positions(token_request, group_lengths, request_count):
    member = (token_request[:, None] == jnp.arange(request_count, dtype=jnp.int32)[None, :]).astype(
        jnp.int32
    )
    earlier = jnp.sum((jnp.cumsum(member, axis=0) - member) * member, axis=1)
    return jnp.sum(member * group_lengths[None, :], axis=1) + earlier


def build_mask(token_request, group_lengths, max_len):
    request_count = group_lengths.shape[0]
    key_index = jnp.arange(request_count * max_len, dtype=jnp.int32)
    key_request = key_index // max_len
    key_alive = key_index % max_len < group_lengths[key_request]
    cached = (token_request[:, None] == key_request[None, :]) & key_alive[None, :]
    token_order = jnp.arange(token_request.shape[0], dtype=jnp.int32)
    fresh = (token_request[:, None] == token_request[None, :]) & (
        token_order[None, :] <= token_order[:, None]
    )
    return jnp.concatenate([cached, fresh], axis=1)


def weigh(scores, allowed):
    masked = jnp.where(allowed, scores, -1e30)
    row_top = jnp.max(masked, axis=-1, keepdims=True)
    exponent = jnp.exp(masked - row_top)
    return (exponent / jnp.sum(exponent, axis=-1, keepdims=True)).astype(jnp.bfloat16)


def on_device(
    tokens, attn_gain, q_weight, k_weight, v_weight, kv_pool, page_table, lengths, token_request
):
    groups = lax.axis_size(GROUP)
    group_idx = lax.axis_index(GROUP)
    mp_idx = lax.axis_index("mp")
    pool_pages = kv_pool.shape[0]
    pair_count = kv_pool.shape[1]
    page_len = kv_pool.shape[3]
    head_dim = kv_pool.shape[4]
    requests_here = lengths.shape[0]
    slot_count = pool_pages // requests_here
    max_len = slot_count * page_len
    capacity = 2 * pool_pages // groups
    flat_table = page_table.reshape(-1)
    slot_ids = jnp.arange(flat_table.shape[0], dtype=jnp.int32)
    held_pages = group_idx * pool_pages + jnp.arange(pool_pages, dtype=jnp.int32)
    held_slots = jnp.sum(
        jnp.where(flat_table[None, :] == held_pages[:, None], slot_ids[None, :], 0), axis=1
    )
    target_owner = held_slots // pool_pages
    owner_hits = (target_owner[:, None] == jnp.arange(groups, dtype=jnp.int32)[None, :]).astype(
        jnp.int32
    )
    order_within = jnp.sum((jnp.cumsum(owner_hits, axis=0) - owner_hits) * owner_hits, axis=1)
    buffer_row = target_owner * capacity + order_within
    page_rows = kv_pool.reshape(pool_pages, -1)
    row_width = page_rows.shape[1]
    buffer_ids = jnp.arange(groups * capacity, dtype=jnp.int32)
    send_pick = (buffer_ids[:, None] == buffer_row[None, :]).astype(jnp.bfloat16)
    outgoing = (
        jnp.dot(send_pick, page_rows, preferred_element_type=jnp.float32)
        .astype(jnp.bfloat16)
        .reshape(groups, capacity, row_width)
    )
    arrived = lax.all_to_all(outgoing, GROUP, split_axis=0, concat_axis=0, tiled=True)
    my_pages = lax.dynamic_slice_in_dim(flat_table, group_idx * pool_pages, pool_pages)
    sender = my_pages // pool_pages
    earlier_same = (sender[None, :] == sender[:, None]) & (my_pages[None, :] < my_pages[:, None])
    arrival_row = sender * capacity + jnp.sum(earlier_same.astype(jnp.int32), axis=1)
    take_pick = (arrival_row[:, None] == buffer_ids[None, :]).astype(jnp.bfloat16)
    placed = jnp.dot(
        take_pick, arrived.reshape(-1, row_width), preferred_element_type=jnp.float32
    ).astype(jnp.bfloat16)
    decoded = placed.reshape(requests_here, slot_count, pair_count, 2, page_len, head_dim)
    decoded = decoded.transpose(0, 2, 3, 1, 4, 5).reshape(
        requests_here, pair_count, 2, max_len, head_dim
    )
    alive_mask = jnp.arange(max_len, dtype=jnp.int32)[None, :] < lengths[:, None]
    decoded = jnp.where(alive_mask[:, None, None, :, None], decoded, jnp.zeros((), jnp.bfloat16))
    whole_rows = gather_by_all_to_all(tokens, "mp", 1)
    normed = normalize(whole_rows, attn_gain)
    rows_here = tokens.shape[0]
    heads_here = q_weight.shape[1] // head_dim
    per_kv = HEADS // KVH
    first_kv = mp_idx * heads_here // per_kv
    is_even = mp_idx % 2 == 0
    kv_weight = jnp.concatenate([k_weight, v_weight], axis=1)
    own_kv_cols = lax.dynamic_slice_in_dim(
        kv_weight, (mp_idx % 2) * k_weight.shape[1] + first_kv * head_dim, head_dim, 1
    )
    q_cols = q_weight.shape[1]
    joined_cols = jnp.concatenate([q_weight, own_kv_cols], axis=1)
    joined_sum = jnp.dot(
        normed,
        lax.all_gather(joined_cols, GROUP, axis=0, tiled=True),
        preferred_element_type=jnp.float32,
    )
    query_sum = joined_sum[:, :q_cols]
    kv_sum = joined_sum[:, q_cols:]
    position = token_positions(token_request, lengths, requests_here)
    queries = rotate(query_sum.reshape(rows_here, heads_here, head_dim), position).astype(
        jnp.bfloat16
    )
    rotated_kv = rotate(kv_sum.reshape(rows_here, 1, head_dim), position)[:, 0]
    own_kv = jnp.where(is_even, rotated_kv, kv_sum).astype(jnp.bfloat16)
    other_kv = from_partner(own_kv, "mp", 0)
    new_keys = jnp.where(is_even, own_kv, other_kv)
    new_values = jnp.where(is_even, other_kv, own_kv)
    allowed = build_mask(token_request, lengths, max_len)
    score_scale = head_dim ** (-0.5)
    partner_cache = from_partner(decoded, "mp", 0)
    layer_zero = jnp.where(is_even, decoded, partner_cache)[:, 0]
    all_keys = jnp.concatenate(
        [layer_zero[:, 0].reshape(requests_here * max_len, head_dim), new_keys], axis=0
    )
    all_values = jnp.concatenate(
        [layer_zero[:, 1].reshape(requests_here * max_len, head_dim), new_values], axis=0
    )

    flat_queries = queries.reshape(rows_here * heads_here, head_dim)
    scores = (
        jnp.einsum("td,nd->tn", flat_queries, all_keys, preferred_element_type=jnp.float32)
        * score_scale
    )
    flat_allowed = jnp.broadcast_to(
        allowed[:, None, :], (rows_here, heads_here, allowed.shape[1])
    ).reshape(rows_here * heads_here, allowed.shape[1])
    attn_probs = weigh(scores, flat_allowed)
    heads_out = jnp.dot(attn_probs, all_values, preferred_element_type=jnp.float32).astype(
        jnp.bfloat16
    )
    attention = heads_out.reshape(rows_here, heads_here * head_dim)
    return (attention, partner_cache)


def split_mesh(mesh):
    devices = mesh.devices
    groups, parts = devices.shape
    try:
        z_of = [d.coords[2] for d in devices[:, 0]]
        inner = next((i for i in range(1, groups) if z_of[i] != z_of[0]), groups)
    except (AttributeError, IndexError, TypeError):
        inner = int(round(groups**0.5))
    return Mesh(devices.reshape(groups // inner, inner, parts), ("gz", "gy", "mp"))


def solution(mesh):
    return jax.shard_map(
        on_device,
        mesh=split_mesh(mesh),
        in_specs=(
            P(GROUP, "mp"),
            P(),
            P(GROUP, "mp"),
            P(GROUP, None),
            P(GROUP, None),
            P(GROUP, "mp", None, None, None),
            P(),
            P(GROUP),
            P(GROUP),
        ),
        out_specs=(P(GROUP, "mp"), P(GROUP, "mp", None, None, None)),
        check_vma=False,
    )
```

```python
import jax
import jax.numpy as jnp
from jax import lax
from jax.sharding import Mesh, PartitionSpec as P

HEADS = 32
KVH = 4
GROUP = ("gz", "gy")


rope_theta = 5000000.0
norm_eps = 1e-05


def from_partner(x, axis, bit):
    return lax.ppermute(x, axis, [(i, i ^ 1 << bit) for i in range(lax.axis_size(axis))])


def gather_by_all_to_all(x, axis, dim):
    count = lax.axis_size(axis)
    spread = jnp.broadcast_to(x[None], (count,) + x.shape)
    ordered = lax.all_to_all(spread, axis, 0, 0, tiled=True)
    ordered = jnp.moveaxis(ordered, 0, dim)
    shape = list(x.shape)
    shape[dim] *= count
    return ordered.reshape(shape)


def rotate(vectors, position):
    half_dim = vectors.shape[-1] // 2
    frequency = rope_theta ** (-(jnp.arange(half_dim, dtype=jnp.float32) / half_dim))
    angles = position.astype(jnp.float32)[:, None, None] * frequency[None, None, :]
    cosine = jnp.cos(angles)
    sine_part = jnp.sin(angles)
    first_half = vectors[..., :half_dim]
    second = vectors[..., half_dim:]
    return jnp.concatenate(
        [first_half * cosine - second * sine_part, second * cosine + first_half * sine_part],
        axis=-1,
    )


def normalize(group_rows, attn_gain):
    features = group_rows.astype(jnp.float32)
    root_mean = jnp.sqrt(jnp.mean(features * features, axis=-1, keepdims=True) + norm_eps)
    return (features / root_mean * attn_gain).astype(jnp.bfloat16)


def token_positions(token_request, group_lengths, request_count):
    member = (token_request[:, None] == jnp.arange(request_count, dtype=jnp.int32)[None, :]).astype(
        jnp.int32
    )
    earlier = jnp.sum((jnp.cumsum(member, axis=0) - member) * member, axis=1)
    return jnp.sum(member * group_lengths[None, :], axis=1) + earlier


def build_mask(token_request, group_lengths, max_len):
    request_count = group_lengths.shape[0]
    key_index = jnp.arange(request_count * max_len, dtype=jnp.int32)
    key_request = key_index // max_len
    key_alive = key_index % max_len < group_lengths[key_request]
    cached = (token_request[:, None] == key_request[None, :]) & key_alive[None, :]
    token_order = jnp.arange(token_request.shape[0], dtype=jnp.int32)
    fresh = (token_request[:, None] == token_request[None, :]) & (
        token_order[None, :] <= token_order[:, None]
    )
    return jnp.concatenate([cached, fresh], axis=1)


def weigh(scores, allowed):
    masked = jnp.where(allowed, scores, -1e30)
    row_top = jnp.max(masked, axis=-1, keepdims=True)
    exponent = jnp.exp(masked - row_top)
    return (exponent / jnp.sum(exponent, axis=-1, keepdims=True)).astype(jnp.bfloat16)


def on_device(
    tokens, attn_gain, q_weight, k_weight, v_weight, kv_pool, page_table, lengths, token_request
):
    groups = lax.axis_size(GROUP)
    group_idx = lax.axis_index(GROUP)
    mp_idx = lax.axis_index("mp")
    pool_pages = kv_pool.shape[0]
    pair_count = kv_pool.shape[1]
    page_len = kv_pool.shape[3]
    head_dim = kv_pool.shape[4]
    requests_here = lengths.shape[0]
    slot_count = pool_pages // requests_here
    max_len = slot_count * page_len
    capacity = 2 * pool_pages // groups
    flat_table = page_table.reshape(-1)
    slot_ids = jnp.arange(flat_table.shape[0], dtype=jnp.int32)
    held_pages = group_idx * pool_pages + jnp.arange(pool_pages, dtype=jnp.int32)
    held_slots = jnp.sum(
        jnp.where(flat_table[None, :] == held_pages[:, None], slot_ids[None, :], 0), axis=1
    )
    target_owner = held_slots // pool_pages
    owner_hits = (target_owner[:, None] == jnp.arange(groups, dtype=jnp.int32)[None, :]).astype(
        jnp.int32
    )
    order_within = jnp.sum((jnp.cumsum(owner_hits, axis=0) - owner_hits) * owner_hits, axis=1)
    buffer_row = target_owner * capacity + order_within
    page_rows = kv_pool.reshape(pool_pages, -1)
    row_width = page_rows.shape[1]
    heads_here = q_weight.shape[1] // head_dim
    per_kv = HEADS // KVH
    first_kv = mp_idx * heads_here // per_kv
    kv_weight = jnp.concatenate([k_weight, v_weight], axis=1)
    own_kv_cols = lax.dynamic_slice_in_dim(
        kv_weight, (mp_idx % 2) * k_weight.shape[1] + first_kv * head_dim, head_dim, 1
    )
    kv_rows = own_kv_cols.reshape(-1, row_width)
    buffer_ids = jnp.arange(groups * capacity, dtype=jnp.int32)
    send_pick = (buffer_ids[:, None] == buffer_row[None, :]).astype(jnp.bfloat16)
    outgoing = (
        jnp.dot(send_pick, page_rows, preferred_element_type=jnp.float32)
        .astype(jnp.bfloat16)
        .reshape(groups, capacity, row_width)
    )
    with_kv = jnp.concatenate(
        [outgoing, jnp.broadcast_to(kv_rows[None], (groups,) + kv_rows.shape)], axis=1
    )
    arrived_all = lax.all_to_all(with_kv, GROUP, split_axis=0, concat_axis=0, tiled=True)
    arrived = arrived_all[:, :capacity]
    kv_full = arrived_all[:, capacity:].reshape(-1, head_dim)
    my_pages = lax.dynamic_slice_in_dim(flat_table, group_idx * pool_pages, pool_pages)
    sender = my_pages // pool_pages
    earlier_same = (sender[None, :] == sender[:, None]) & (my_pages[None, :] < my_pages[:, None])
    arrival_row = sender * capacity + jnp.sum(earlier_same.astype(jnp.int32), axis=1)
    take_pick = (arrival_row[:, None] == buffer_ids[None, :]).astype(jnp.bfloat16)
    placed = jnp.dot(
        take_pick, arrived.reshape(-1, row_width), preferred_element_type=jnp.float32
    ).astype(jnp.bfloat16)
    decoded = placed.reshape(requests_here, slot_count, pair_count, 2, page_len, head_dim)
    decoded = decoded.transpose(0, 2, 3, 1, 4, 5).reshape(
        requests_here, pair_count, 2, max_len, head_dim
    )
    alive_mask = jnp.arange(max_len, dtype=jnp.int32)[None, :] < lengths[:, None]
    decoded = jnp.where(alive_mask[:, None, None, :, None], decoded, jnp.zeros((), jnp.bfloat16))
    whole_rows = gather_by_all_to_all(tokens, "mp", 1)
    normed = normalize(whole_rows, attn_gain)
    rows_here = tokens.shape[0]
    is_even = mp_idx % 2 == 0
    kv_sum = jnp.dot(normed, kv_full, preferred_element_type=jnp.float32)
    query_sum = jnp.dot(
        normed,
        lax.all_gather(q_weight, GROUP, axis=0, tiled=True),
        preferred_element_type=jnp.float32,
    )
    position = token_positions(token_request, lengths, requests_here)
    queries = rotate(query_sum.reshape(rows_here, heads_here, head_dim), position).astype(
        jnp.bfloat16
    )
    rotated_kv = rotate(kv_sum.reshape(rows_here, 1, head_dim), position)[:, 0]
    own_kv = jnp.where(is_even, rotated_kv, kv_sum).astype(jnp.bfloat16)
    other_kv = from_partner(own_kv, "mp", 0)
    new_keys = jnp.where(is_even, own_kv, other_kv)
    new_values = jnp.where(is_even, other_kv, own_kv)
    allowed = build_mask(token_request, lengths, max_len)
    score_scale = head_dim ** (-0.5)
    partner_cache = from_partner(decoded, "mp", 0)
    layer_zero = jnp.where(is_even, decoded, partner_cache)[:, 0]
    all_keys = jnp.concatenate(
        [layer_zero[:, 0].reshape(requests_here * max_len, head_dim), new_keys], axis=0
    )
    all_values = jnp.concatenate(
        [layer_zero[:, 1].reshape(requests_here * max_len, head_dim), new_values], axis=0
    )

    flat_queries = queries.reshape(rows_here * heads_here, head_dim)
    scores = (
        jnp.einsum("td,nd->tn", flat_queries, all_keys, preferred_element_type=jnp.float32)
        * score_scale
    )
    flat_allowed = jnp.broadcast_to(
        allowed[:, None, :], (rows_here, heads_here, allowed.shape[1])
    ).reshape(rows_here * heads_here, allowed.shape[1])
    attn_probs = weigh(scores, flat_allowed)
    heads_out = jnp.dot(attn_probs, all_values, preferred_element_type=jnp.float32).astype(
        jnp.bfloat16
    )
    attention = heads_out.reshape(rows_here, heads_here * head_dim)
    return (attention, partner_cache)


def split_mesh(mesh):
    devices = mesh.devices
    groups, parts = devices.shape
    try:
        z_of = [d.coords[2] for d in devices[:, 0]]
        inner = next((i for i in range(1, groups) if z_of[i] != z_of[0]), groups)
    except (AttributeError, IndexError, TypeError):
        inner = int(round(groups**0.5))
    return Mesh(devices.reshape(groups // inner, inner, parts), ("gz", "gy", "mp"))


def solution(mesh):
    return jax.shard_map(
        on_device,
        mesh=split_mesh(mesh),
        in_specs=(
            P(GROUP, "mp"),
            P(),
            P(GROUP, "mp"),
            P(GROUP, None),
            P(GROUP, None),
            P(GROUP, "mp", None, None, None),
            P(),
            P(GROUP),
            P(GROUP),
        ),
        out_specs=(P(GROUP, "mp"), P(GROUP, "mp", None, None, None)),
        check_vma=False,
    )
```

```python
import jax
import jax.numpy as jnp
from jax import lax
from jax.sharding import Mesh, PartitionSpec as P

HEADS = 32
KVH = 4
GROUP = ("gz", "gy")


rope_theta = 5000000.0
norm_eps = 1e-05


def from_partner(x, axis, bit):
    return lax.ppermute(x, axis, [(i, i ^ 1 << bit) for i in range(lax.axis_size(axis))])


def gather_by_all_to_all(x, axis, dim):
    count = lax.axis_size(axis)
    spread = jnp.broadcast_to(x[None], (count,) + x.shape)
    ordered = lax.all_to_all(spread, axis, 0, 0, tiled=True)
    ordered = jnp.moveaxis(ordered, 0, dim)
    shape = list(x.shape)
    shape[dim] *= count
    return ordered.reshape(shape)


def rotate(vectors, position):
    half_dim = vectors.shape[-1] // 2
    frequency = rope_theta ** (-(jnp.arange(half_dim, dtype=jnp.float32) / half_dim))
    angles = position.astype(jnp.float32)[:, None, None] * frequency[None, None, :]
    cosine = jnp.cos(angles)
    sine_part = jnp.sin(angles)
    first_half = vectors[..., :half_dim]
    second = vectors[..., half_dim:]
    return jnp.concatenate(
        [first_half * cosine - second * sine_part, second * cosine + first_half * sine_part],
        axis=-1,
    )


def normalize(group_rows, attn_gain):
    features = group_rows.astype(jnp.float32)
    root_mean = jnp.sqrt(jnp.mean(features * features, axis=-1, keepdims=True) + norm_eps)
    return (features / root_mean * attn_gain).astype(jnp.bfloat16)


def token_positions(token_request, group_lengths, request_count):
    member = (token_request[:, None] == jnp.arange(request_count, dtype=jnp.int32)[None, :]).astype(
        jnp.int32
    )
    earlier = jnp.sum((jnp.cumsum(member, axis=0) - member) * member, axis=1)
    return jnp.sum(member * group_lengths[None, :], axis=1) + earlier


def build_mask(token_request, group_lengths, max_len):
    request_count = group_lengths.shape[0]
    key_index = jnp.arange(request_count * max_len, dtype=jnp.int32)
    key_request = key_index // max_len
    key_alive = key_index % max_len < group_lengths[key_request]
    cached = (token_request[:, None] == key_request[None, :]) & key_alive[None, :]
    token_order = jnp.arange(token_request.shape[0], dtype=jnp.int32)
    fresh = (token_request[:, None] == token_request[None, :]) & (
        token_order[None, :] <= token_order[:, None]
    )
    return jnp.concatenate([cached, fresh], axis=1)


def weigh(scores, allowed):
    masked = jnp.where(allowed, scores, -1e30)
    row_top = jnp.max(masked, axis=-1, keepdims=True)
    exponent = jnp.exp(masked - row_top)
    return (exponent / jnp.sum(exponent, axis=-1, keepdims=True)).astype(jnp.bfloat16)


def on_device(
    tokens, attn_gain, q_weight, k_weight, v_weight, kv_pool, page_table, lengths, token_request
):
    groups = lax.axis_size(GROUP)
    group_idx = lax.axis_index(GROUP)
    mp_idx = lax.axis_index("mp")
    pool_pages = kv_pool.shape[0]
    pair_count = kv_pool.shape[1]
    page_len = kv_pool.shape[3]
    head_dim = kv_pool.shape[4]
    requests_here = lengths.shape[0]
    slot_count = pool_pages // requests_here
    max_len = slot_count * page_len
    capacity = 2 * pool_pages // groups
    flat_table = page_table.reshape(-1)
    slot_ids = jnp.arange(flat_table.shape[0], dtype=jnp.int32)
    held_pages = group_idx * pool_pages + jnp.arange(pool_pages, dtype=jnp.int32)
    held_slots = jnp.sum(
        jnp.where(flat_table[None, :] == held_pages[:, None], slot_ids[None, :], 0), axis=1
    )
    target_owner = held_slots // pool_pages
    owner_hits = (target_owner[:, None] == jnp.arange(groups, dtype=jnp.int32)[None, :]).astype(
        jnp.int32
    )
    order_within = jnp.sum((jnp.cumsum(owner_hits, axis=0) - owner_hits) * owner_hits, axis=1)
    buffer_row = target_owner * capacity + order_within
    page_rows = kv_pool.reshape(pool_pages, -1)
    row_width = page_rows.shape[1]
    buffer_ids = jnp.arange(groups * capacity, dtype=jnp.int32)
    send_pick = (buffer_ids[:, None] == buffer_row[None, :]).astype(jnp.bfloat16)
    outgoing = (
        jnp.dot(send_pick, page_rows, preferred_element_type=jnp.float32)
        .astype(jnp.bfloat16)
        .reshape(groups, capacity, row_width)
    )
    arrived = lax.all_to_all(outgoing, GROUP, split_axis=0, concat_axis=0, tiled=True)
    my_pages = lax.dynamic_slice_in_dim(flat_table, group_idx * pool_pages, pool_pages)
    sender = my_pages // pool_pages
    earlier_same = (sender[None, :] == sender[:, None]) & (my_pages[None, :] < my_pages[:, None])
    arrival_row = sender * capacity + jnp.sum(earlier_same.astype(jnp.int32), axis=1)
    take_pick = (arrival_row[:, None] == buffer_ids[None, :]).astype(jnp.bfloat16)
    placed = jnp.dot(
        take_pick, arrived.reshape(-1, row_width), preferred_element_type=jnp.float32
    ).astype(jnp.bfloat16)
    decoded = placed.reshape(requests_here, slot_count, pair_count, 2, page_len, head_dim)
    decoded = decoded.transpose(0, 2, 3, 1, 4, 5).reshape(
        requests_here, pair_count, 2, max_len, head_dim
    )
    alive_mask = jnp.arange(max_len, dtype=jnp.int32)[None, :] < lengths[:, None]
    decoded = jnp.where(alive_mask[:, None, None, :, None], decoded, jnp.zeros((), jnp.bfloat16))
    whole_rows = gather_by_all_to_all(tokens, "mp", 1)
    normed = normalize(whole_rows, attn_gain)
    rows_here = tokens.shape[0]
    heads_here = q_weight.shape[1] // head_dim
    per_kv = HEADS // KVH
    first_kv = mp_idx * heads_here // per_kv
    is_even = mp_idx % 2 == 0
    own_kv_cols = lax.dynamic_slice_in_dim(
        jnp.where(is_even, k_weight, v_weight), first_kv * head_dim, head_dim, 1
    )
    q_cols = q_weight.shape[1]
    joined_cols = jnp.concatenate([q_weight, own_kv_cols], axis=1)
    joined_sum = jnp.dot(
        normed,
        lax.all_gather(joined_cols, GROUP, axis=0, tiled=True),
        preferred_element_type=jnp.float32,
    )
    query_sum = joined_sum[:, :q_cols]
    kv_sum = joined_sum[:, q_cols:]
    position = token_positions(token_request, lengths, requests_here)
    queries = rotate(query_sum.reshape(rows_here, heads_here, head_dim), position).astype(
        jnp.bfloat16
    )
    rotated_kv = rotate(kv_sum.reshape(rows_here, 1, head_dim), position)[:, 0]
    own_kv = jnp.where(is_even, rotated_kv, kv_sum).astype(jnp.bfloat16)
    other_kv = from_partner(own_kv, "mp", 0)
    new_keys = jnp.where(is_even, own_kv, other_kv)
    new_values = jnp.where(is_even, other_kv, own_kv)
    allowed = build_mask(token_request, lengths, max_len)
    score_scale = head_dim ** (-0.5)
    partner_cache = from_partner(decoded, "mp", 0)
    layer_zero = jnp.where(is_even, decoded, partner_cache)[:, 0]
    cache_keys = layer_zero[:, 0].reshape(requests_here * max_len, head_dim)
    all_values = jnp.concatenate(
        [layer_zero[:, 1].reshape(requests_here * max_len, head_dim), new_values], axis=0
    )
    flat_queries = queries.reshape(rows_here * heads_here, head_dim)
    cache_scores = jnp.einsum(
        "td,nd->tn", flat_queries, cache_keys, preferred_element_type=jnp.float32
    )
    fresh_scores = jnp.einsum(
        "td,nd->tn", flat_queries, new_keys, preferred_element_type=jnp.float32
    )
    scores = jnp.concatenate([cache_scores, fresh_scores], axis=1) * score_scale
    flat_allowed = jnp.broadcast_to(
        allowed[:, None, :], (rows_here, heads_here, allowed.shape[1])
    ).reshape(rows_here * heads_here, allowed.shape[1])
    attn_probs = weigh(scores, flat_allowed)
    heads_out = jnp.dot(attn_probs, all_values, preferred_element_type=jnp.float32).astype(
        jnp.bfloat16
    )
    attention = heads_out.reshape(rows_here, heads_here * head_dim)
    return (attention, partner_cache)


def split_mesh(mesh):
    devices = mesh.devices
    groups, parts = devices.shape
    try:
        z_of = [d.coords[2] for d in devices[:, 0]]
        inner = next((i for i in range(1, groups) if z_of[i] != z_of[0]), groups)
    except (AttributeError, IndexError, TypeError):
        inner = int(round(groups**0.5))
    return Mesh(devices.reshape(groups // inner, inner, parts), ("gz", "gy", "mp"))


def solution(mesh):
    return jax.shard_map(
        on_device,
        mesh=split_mesh(mesh),
        in_specs=(
            P(GROUP, "mp"),
            P(),
            P(GROUP, "mp"),
            P(GROUP, None),
            P(GROUP, None),
            P(GROUP, "mp", None, None, None),
            P(),
            P(GROUP),
            P(GROUP),
        ),
        out_specs=(P(GROUP, "mp"), P(GROUP, "mp", None, None, None)),
        check_vma=False,
    )
```

```python
import jax
import jax.numpy as jnp
from jax import lax
from jax.experimental import pallas as pl
from jax.sharding import Mesh, PartitionSpec as P

HEADS = 32
KVH = 4
GROUP = ("gz", "gy")


rope_theta = 5000000.0
norm_eps = 1e-05


def from_partner(x, axis, bit):
    return lax.ppermute(x, axis, [(i, i ^ 1 << bit) for i in range(lax.axis_size(axis))])


def gather_by_all_to_all(x, axis, dim):
    count = lax.axis_size(axis)
    spread = jnp.broadcast_to(x[None], (count,) + x.shape)
    ordered = lax.all_to_all(spread, axis, 0, 0, tiled=True)
    ordered = jnp.moveaxis(ordered, 0, dim)
    shape = list(x.shape)
    shape[dim] *= count
    return ordered.reshape(shape)


def project_kernel(rows_ref, weight_ref, out_ref):
    @pl.when(pl.program_id(0) == 0)
    def _():
        out_ref[...] = jnp.zeros_like(out_ref)

    out_ref[...] += jnp.dot(rows_ref[...], weight_ref[...], preferred_element_type=jnp.float32)


def project(rows, weight, block=512):
    steps = weight.shape[0] // block
    return pl.pallas_call(
        project_kernel,
        grid=(steps,),
        in_specs=[
            pl.BlockSpec((rows.shape[0], block), lambda k: (0, k)),
            pl.BlockSpec((block, weight.shape[1]), lambda k: (k, 0)),
        ],
        out_specs=pl.BlockSpec((rows.shape[0], weight.shape[1]), lambda k: (0, 0)),
        out_shape=jax.ShapeDtypeStruct((rows.shape[0], weight.shape[1]), jnp.float32),
    )(rows, weight)


def rotate(vectors, position):
    half_dim = vectors.shape[-1] // 2
    frequency = rope_theta ** (-(jnp.arange(half_dim, dtype=jnp.float32) / half_dim))
    angles = position.astype(jnp.float32)[:, None, None] * frequency[None, None, :]
    cosine = jnp.cos(angles)
    sine_part = jnp.sin(angles)
    first_half = vectors[..., :half_dim]
    second = vectors[..., half_dim:]
    return jnp.concatenate(
        [first_half * cosine - second * sine_part, second * cosine + first_half * sine_part],
        axis=-1,
    )


def normalize(group_rows, attn_gain):
    features = group_rows.astype(jnp.float32)
    root_mean = jnp.sqrt(jnp.mean(features * features, axis=-1, keepdims=True) + norm_eps)
    return (features / root_mean * attn_gain).astype(jnp.bfloat16)


def token_positions(token_request, group_lengths, request_count):
    member = (token_request[:, None] == jnp.arange(request_count, dtype=jnp.int32)[None, :]).astype(
        jnp.int32
    )
    earlier = jnp.sum((jnp.cumsum(member, axis=0) - member) * member, axis=1)
    return jnp.sum(member * group_lengths[None, :], axis=1) + earlier


def build_mask(token_request, group_lengths, max_len):
    request_count = group_lengths.shape[0]
    key_index = jnp.arange(request_count * max_len, dtype=jnp.int32)
    key_request = key_index // max_len
    key_alive = key_index % max_len < group_lengths[key_request]
    cached = (token_request[:, None] == key_request[None, :]) & key_alive[None, :]
    token_order = jnp.arange(token_request.shape[0], dtype=jnp.int32)
    fresh = (token_request[:, None] == token_request[None, :]) & (
        token_order[None, :] <= token_order[:, None]
    )
    return jnp.concatenate([cached, fresh], axis=1)


def weigh(scores, allowed):
    masked = jnp.where(allowed, scores, -1e30)
    row_top = jnp.max(masked, axis=-1, keepdims=True)
    exponent = jnp.exp(masked - row_top)
    return (exponent / jnp.sum(exponent, axis=-1, keepdims=True)).astype(jnp.bfloat16)


def on_device(
    tokens, attn_gain, q_weight, k_weight, v_weight, kv_pool, page_table, lengths, token_request
):
    groups = lax.axis_size(GROUP)
    group_idx = lax.axis_index(GROUP)
    mp_idx = lax.axis_index("mp")
    pool_pages = kv_pool.shape[0]
    pair_count = kv_pool.shape[1]
    page_len = kv_pool.shape[3]
    head_dim = kv_pool.shape[4]
    requests_here = lengths.shape[0]
    slot_count = pool_pages // requests_here
    max_len = slot_count * page_len
    capacity = 2 * pool_pages // groups
    flat_table = page_table.reshape(-1)
    slot_ids = jnp.arange(flat_table.shape[0], dtype=jnp.int32)
    held_pages = group_idx * pool_pages + jnp.arange(pool_pages, dtype=jnp.int32)
    held_slots = jnp.sum(
        jnp.where(flat_table[None, :] == held_pages[:, None], slot_ids[None, :], 0), axis=1
    )
    target_owner = held_slots // pool_pages
    owner_hits = (target_owner[:, None] == jnp.arange(groups, dtype=jnp.int32)[None, :]).astype(
        jnp.int32
    )
    order_within = jnp.sum((jnp.cumsum(owner_hits, axis=0) - owner_hits) * owner_hits, axis=1)
    buffer_row = target_owner * capacity + order_within
    page_rows = kv_pool.reshape(pool_pages, -1)
    row_width = page_rows.shape[1]
    buffer_ids = jnp.arange(groups * capacity, dtype=jnp.int32)
    send_pick = (buffer_ids[:, None] == buffer_row[None, :]).astype(jnp.bfloat16)
    outgoing = (
        jnp.dot(send_pick, page_rows, preferred_element_type=jnp.float32)
        .astype(jnp.bfloat16)
        .reshape(groups, capacity, row_width)
    )
    arrived = lax.all_to_all(outgoing, GROUP, split_axis=0, concat_axis=0, tiled=True)
    my_pages = lax.dynamic_slice_in_dim(flat_table, group_idx * pool_pages, pool_pages)
    sender = my_pages // pool_pages
    earlier_same = (sender[None, :] == sender[:, None]) & (my_pages[None, :] < my_pages[:, None])
    arrival_row = sender * capacity + jnp.sum(earlier_same.astype(jnp.int32), axis=1)
    take_pick = (arrival_row[:, None] == buffer_ids[None, :]).astype(jnp.bfloat16)
    placed = jnp.dot(
        take_pick, arrived.reshape(-1, row_width), preferred_element_type=jnp.float32
    ).astype(jnp.bfloat16)
    decoded = placed.reshape(requests_here, slot_count, pair_count, 2, page_len, head_dim)
    decoded = decoded.transpose(0, 2, 3, 1, 4, 5).reshape(
        requests_here, pair_count, 2, max_len, head_dim
    )
    alive_mask = jnp.arange(max_len, dtype=jnp.int32)[None, :] < lengths[:, None]
    decoded = jnp.where(alive_mask[:, None, None, :, None], decoded, jnp.zeros((), jnp.bfloat16))
    whole_rows = gather_by_all_to_all(tokens, "mp", 1)
    normed = normalize(whole_rows, attn_gain)
    rows_here = tokens.shape[0]
    heads_here = q_weight.shape[1] // head_dim
    per_kv = HEADS // KVH
    first_kv = mp_idx * heads_here // per_kv
    is_even = mp_idx % 2 == 0
    kv_weight = jnp.concatenate([k_weight, v_weight], axis=1)
    own_kv_cols = lax.dynamic_slice_in_dim(
        kv_weight, (mp_idx % 2) * k_weight.shape[1] + first_kv * head_dim, head_dim, 1
    )
    q_cols = q_weight.shape[1]
    joined_cols = jnp.concatenate([q_weight, own_kv_cols], axis=1)
    joined_sum = project(normed, lax.all_gather(joined_cols, GROUP, axis=0, tiled=True))
    query_sum = joined_sum[:, :q_cols]
    kv_sum = joined_sum[:, q_cols:]
    position = token_positions(token_request, lengths, requests_here)
    queries = rotate(query_sum.reshape(rows_here, heads_here, head_dim), position).astype(
        jnp.bfloat16
    )
    rotated_kv = rotate(kv_sum.reshape(rows_here, 1, head_dim), position)[:, 0]
    own_kv = jnp.where(is_even, rotated_kv, kv_sum).astype(jnp.bfloat16)
    other_kv = from_partner(own_kv, "mp", 0)
    new_keys = jnp.where(is_even, own_kv, other_kv)
    new_values = jnp.where(is_even, other_kv, own_kv)
    allowed = build_mask(token_request, lengths, max_len)
    score_scale = head_dim ** (-0.5)
    partner_cache = from_partner(decoded, "mp", 0)
    layer_zero = jnp.where(is_even, decoded, partner_cache)[:, 0]
    all_keys = jnp.concatenate(
        [layer_zero[:, 0].reshape(requests_here * max_len, head_dim), new_keys], axis=0
    )
    all_values = jnp.concatenate(
        [layer_zero[:, 1].reshape(requests_here * max_len, head_dim), new_values], axis=0
    )

    flat_queries = queries.reshape(rows_here * heads_here, head_dim)
    scores = (
        jnp.einsum("td,nd->tn", flat_queries, all_keys, preferred_element_type=jnp.float32)
        * score_scale
    )
    flat_allowed = jnp.broadcast_to(
        allowed[:, None, :], (rows_here, heads_here, allowed.shape[1])
    ).reshape(rows_here * heads_here, allowed.shape[1])
    attn_probs = weigh(scores, flat_allowed)
    heads_out = jnp.dot(attn_probs, all_values, preferred_element_type=jnp.float32).astype(
        jnp.bfloat16
    )
    attention = heads_out.reshape(rows_here, heads_here * head_dim)
    return (attention, partner_cache)


def split_mesh(mesh):
    devices = mesh.devices
    groups, parts = devices.shape
    try:
        z_of = [d.coords[2] for d in devices[:, 0]]
        inner = next((i for i in range(1, groups) if z_of[i] != z_of[0]), groups)
    except (AttributeError, IndexError, TypeError):
        inner = int(round(groups**0.5))
    return Mesh(devices.reshape(groups // inner, inner, parts), ("gz", "gy", "mp"))


def solution(mesh):
    return jax.shard_map(
        on_device,
        mesh=split_mesh(mesh),
        in_specs=(
            P(GROUP, "mp"),
            P(),
            P(GROUP, "mp"),
            P(GROUP, None),
            P(GROUP, None),
            P(GROUP, "mp", None, None, None),
            P(),
            P(GROUP),
            P(GROUP),
        ),
        out_specs=(P(GROUP, "mp"), P(GROUP, "mp", None, None, None)),
        check_vma=False,
    )
```

```python
import jax
import jax.numpy as jnp
from jax import lax
from jax.sharding import Mesh, PartitionSpec as P

HEADS = 32
KVH = 4
GROUP = ("gz", "gy")


rope_theta = 5000000.0
norm_eps = 1e-05


def from_partner(x, axis, bit):
    return lax.ppermute(x, axis, [(i, i ^ 1 << bit) for i in range(lax.axis_size(axis))])


def gather_by_all_to_all(x, axis, dim):
    count = lax.axis_size(axis)
    spread = jnp.broadcast_to(x[None], (count,) + x.shape)
    ordered = lax.all_to_all(spread, axis, 0, 0, tiled=True)
    ordered = jnp.moveaxis(ordered, 0, dim)
    shape = list(x.shape)
    shape[dim] *= count
    return ordered.reshape(shape)


def rotate(vectors, position):
    half_dim = vectors.shape[-1] // 2
    frequency = rope_theta ** (-(jnp.arange(half_dim, dtype=jnp.float32) / half_dim))
    angles = position.astype(jnp.float32)[:, None, None] * frequency[None, None, :]
    cosine = jnp.cos(angles)
    sine_part = jnp.sin(angles)
    first_half = vectors[..., :half_dim]
    second = vectors[..., half_dim:]
    return jnp.concatenate(
        [first_half * cosine - second * sine_part, second * cosine + first_half * sine_part],
        axis=-1,
    )


def normalize(group_rows, attn_gain):
    features = group_rows.astype(jnp.float32)
    root_mean = jnp.sqrt(jnp.mean(features * features, axis=-1, keepdims=True) + norm_eps)
    return (features / root_mean * attn_gain).astype(jnp.bfloat16)


def token_positions(token_request, group_lengths, request_count):
    member = (token_request[:, None] == jnp.arange(request_count, dtype=jnp.int32)[None, :]).astype(
        jnp.int32
    )
    earlier = jnp.sum((jnp.cumsum(member, axis=0) - member) * member, axis=1)
    return jnp.sum(member * group_lengths[None, :], axis=1) + earlier


def build_mask(token_request, group_lengths, max_len):
    request_count = group_lengths.shape[0]
    key_index = jnp.arange(request_count * max_len, dtype=jnp.int32)
    key_request = key_index // max_len
    key_alive = key_index % max_len < group_lengths[key_request]
    cached = (token_request[:, None] == key_request[None, :]) & key_alive[None, :]
    token_order = jnp.arange(token_request.shape[0], dtype=jnp.int32)
    fresh = (token_request[:, None] == token_request[None, :]) & (
        token_order[None, :] <= token_order[:, None]
    )
    return jnp.concatenate([cached, fresh], axis=1)


def weigh(scores, allowed):
    masked = jnp.where(allowed, scores, -1e30)
    row_top = jnp.max(masked, axis=-1, keepdims=True)
    exponent = jnp.exp(masked - row_top)
    return (exponent / jnp.sum(exponent, axis=-1, keepdims=True)).astype(jnp.bfloat16)


def on_device(
    tokens, attn_gain, q_weight, k_weight, v_weight, kv_pool, page_table, lengths, token_request
):
    groups = lax.axis_size(GROUP)
    group_idx = lax.axis_index(GROUP)
    mp_idx = lax.axis_index("mp")
    pool_pages = kv_pool.shape[0]
    pair_count = kv_pool.shape[1]
    page_len = kv_pool.shape[3]
    head_dim = kv_pool.shape[4]
    requests_here = lengths.shape[0]
    slot_count = pool_pages // requests_here
    max_len = slot_count * page_len
    capacity = 2 * pool_pages // groups
    flat_table = page_table.reshape(-1)
    slot_ids = jnp.arange(flat_table.shape[0], dtype=jnp.int32)
    held_pages = group_idx * pool_pages + jnp.arange(pool_pages, dtype=jnp.int32)
    held_slots = jnp.sum(
        jnp.where(flat_table[None, :] == held_pages[:, None], slot_ids[None, :], 0), axis=1
    )
    target_owner = held_slots // pool_pages
    owner_hits = (target_owner[:, None] == jnp.arange(groups, dtype=jnp.int32)[None, :]).astype(
        jnp.int32
    )
    order_within = jnp.sum((jnp.cumsum(owner_hits, axis=0) - owner_hits) * owner_hits, axis=1)
    buffer_row = target_owner * capacity + order_within
    page_rows = kv_pool.reshape(pool_pages, -1)
    row_width = page_rows.shape[1]
    buffer_ids = jnp.arange(groups * capacity, dtype=jnp.int32)
    send_pick = (buffer_ids[:, None] == buffer_row[None, :]).astype(jnp.bfloat16)
    outgoing = (
        jnp.dot(send_pick, page_rows, preferred_element_type=jnp.float32)
        .astype(jnp.bfloat16)
        .reshape(groups, capacity, row_width)
    )
    arrived = lax.all_to_all(outgoing, GROUP, split_axis=0, concat_axis=0, tiled=True)
    my_pages = lax.dynamic_slice_in_dim(flat_table, group_idx * pool_pages, pool_pages)
    sender = my_pages // pool_pages
    earlier_same = (sender[None, :] == sender[:, None]) & (my_pages[None, :] < my_pages[:, None])
    arrival_row = sender * capacity + jnp.sum(earlier_same.astype(jnp.int32), axis=1)
    take_pick = (arrival_row[:, None] == buffer_ids[None, :]).astype(jnp.bfloat16)
    placed = jnp.dot(
        take_pick, arrived.reshape(-1, row_width), preferred_element_type=jnp.float32
    ).astype(jnp.bfloat16)
    decoded = placed.reshape(requests_here, slot_count, pair_count, 2, page_len, head_dim)
    decoded = decoded.transpose(0, 2, 3, 1, 4, 5).reshape(
        requests_here, pair_count, 2, max_len, head_dim
    )
    alive_mask = jnp.arange(max_len, dtype=jnp.int32)[None, :] < lengths[:, None]
    raw_decoded = decoded
    decoded = jnp.where(alive_mask[:, None, None, :, None], decoded, jnp.zeros((), jnp.bfloat16))
    whole_rows = gather_by_all_to_all(tokens, "mp", 1)
    normed = normalize(whole_rows, attn_gain)
    rows_here = tokens.shape[0]
    heads_here = q_weight.shape[1] // head_dim
    per_kv = HEADS // KVH
    first_kv = mp_idx * heads_here // per_kv
    is_even = mp_idx % 2 == 0
    kv_weight = jnp.concatenate([k_weight, v_weight], axis=1)
    own_kv_cols = lax.dynamic_slice_in_dim(
        kv_weight, (mp_idx % 2) * k_weight.shape[1] + first_kv * head_dim, head_dim, 1
    )
    q_cols = q_weight.shape[1]
    joined_cols = jnp.concatenate([q_weight, own_kv_cols], axis=1)
    joined_sum = jnp.dot(
        normed,
        lax.all_gather(joined_cols, GROUP, axis=0, tiled=True),
        preferred_element_type=jnp.float32,
    )
    query_sum = joined_sum[:, :q_cols]
    kv_sum = joined_sum[:, q_cols:]
    position = token_positions(token_request, lengths, requests_here)
    queries = rotate(query_sum.reshape(rows_here, heads_here, head_dim), position).astype(
        jnp.bfloat16
    )
    rotated_kv = rotate(kv_sum.reshape(rows_here, 1, head_dim), position)[:, 0]
    own_kv = jnp.where(is_even, rotated_kv, kv_sum).astype(jnp.bfloat16)
    other_kv = from_partner(own_kv, "mp", 0)
    new_keys = jnp.where(is_even, own_kv, other_kv)
    new_values = jnp.where(is_even, other_kv, own_kv)
    allowed = build_mask(token_request, lengths, max_len)
    score_scale = head_dim ** (-0.5)
    partner_cache = jnp.where(
        alive_mask[:, None, None, :, None],
        from_partner(raw_decoded, "mp", 0),
        jnp.zeros((), jnp.bfloat16),
    )
    layer_zero = jnp.where(is_even, decoded, partner_cache)[:, 0]
    all_keys = jnp.concatenate(
        [layer_zero[:, 0].reshape(requests_here * max_len, head_dim), new_keys], axis=0
    )
    all_values = jnp.concatenate(
        [layer_zero[:, 1].reshape(requests_here * max_len, head_dim), new_values], axis=0
    )

    flat_queries = queries.reshape(rows_here * heads_here, head_dim)
    scores = (
        jnp.einsum("td,nd->tn", flat_queries, all_keys, preferred_element_type=jnp.float32)
        * score_scale
    )
    flat_allowed = jnp.broadcast_to(
        allowed[:, None, :], (rows_here, heads_here, allowed.shape[1])
    ).reshape(rows_here * heads_here, allowed.shape[1])
    attn_probs = weigh(scores, flat_allowed)
    heads_out = jnp.dot(attn_probs, all_values, preferred_element_type=jnp.float32).astype(
        jnp.bfloat16
    )
    attention = heads_out.reshape(rows_here, heads_here * head_dim)
    return (attention, partner_cache)


def split_mesh(mesh):
    devices = mesh.devices
    groups, parts = devices.shape
    try:
        z_of = [d.coords[2] for d in devices[:, 0]]
        inner = next((i for i in range(1, groups) if z_of[i] != z_of[0]), groups)
    except (AttributeError, IndexError, TypeError):
        inner = int(round(groups**0.5))
    return Mesh(devices.reshape(groups // inner, inner, parts), ("gz", "gy", "mp"))


def solution(mesh):
    return jax.shard_map(
        on_device,
        mesh=split_mesh(mesh),
        in_specs=(
            P(GROUP, "mp"),
            P(),
            P(GROUP, "mp"),
            P(GROUP, None),
            P(GROUP, None),
            P(GROUP, "mp", None, None, None),
            P(),
            P(GROUP),
            P(GROUP),
        ),
        out_specs=(P(GROUP, "mp"), P(GROUP, "mp", None, None, None)),
        check_vma=False,
    )
```
